768 devices in a mesh: rad: 12 (over z_lo, core), azi: 64 (over z_hi, x, y).
Axes of the slice: x: 4, y: 8, z: 12 (z_hi: 2, z_lo: 6; z = z_hi * 6 + z_lo), core: 2. Of those that a mesh axis runs over, the one named last changes fastest.
Arguments:
- fields: float32 [3, 8, 96, 8192], P(None, None, 'rad', 'azi'), may hold values from -6 to 6
- viscosity: float32 [96, 8192], P('rad', 'azi'), may hold values from 0.05 to 0.5
- rotation: float32 [96], replicated, may hold values from 0.2 to 2
- shift_blocks: int32 [1, 96], replicated, may hold values from 0 to 127
Outputs:
- fields_out: float32 [3, 8, 96, 8192], P(None, None, 'rad', 'azi')
The draws below stay inside these ranges and needn't reach their ends.
Inputs may be any that keep to these rules, and one draw needn't show every extreme that they name: `shift_blocks`: shift of radius r after step t, in blocks of 64 azimuth cells.
All inputs are finite; a program needn't handle non-finite values.
Results may differ from the reference program's by a relative error of at most 0.00002.
Values sent between devices are 32-bit elements; how exact they have to be, the bound alone decides.
No kernel may reach another device: no remote copies, remote signals or barrier semaphores. Data moves between devices by JAX's collectives and lax.ppermute only.
A program may use at most 32 MiB of HBM per device.

```python
import math
import jax
import jax.numpy as jnp
from jax import lax

H = 8
BLOCK = 64
STEPS = 1
NR = 96
NA = 8192
NB = 128


def place_ends(values, stream_key, smallest, top_value):
    place = [jax.random.randint(jax.random.fold_in(stream_key, axis), (), 0, length) for axis, length in enumerate(values.shape)]
    main_axis = values.shape.index(max(values.shape))
    neighbour = place[:main_axis] + [(place[main_axis] + 1) % values.shape[main_axis]] + place[main_axis + 1:]
    return values.at[tuple(place)].set(smallest).at[tuple(neighbour)].set(top_value)


def steps_of(own_key, extent, pieces, least, largest):
    loudness = 1.0
    for position, parts in pieces:
        steps = jax.random.uniform(jax.random.fold_in(jax.random.fold_in(own_key, 6), position), (parts,), jnp.float32, least / len(pieces), largest / len(pieces))
        loudness = loudness * jnp.repeat(jnp.exp(steps), extent[position] // parts).reshape((-1,) + (1,) * (len(extent) - 1 - position))
    return loudness


def noise(stream_key, shape, scale, reach, shards=(), dtype=jnp.bfloat16):
    drawn = scale * jax.random.normal(stream_key, shape, jnp.float32)
    if shards:
        drawn = drawn * steps_of(stream_key, shape, shards, -0.22, 0.18)
    return jnp.clip(drawn, -reach, reach).astype(dtype)


def setup_inputs(seed: int = 0) -> dict:
    keys = jax.random.split(jax.random.key(seed), 5)
    fields = noise(keys[0], (3, H, NR, NA), 1.0, 6.0, ((2, 12), (3, 64)), jnp.float32)
    viscosity = jnp.clip(jnp.exp(math.log(0.5) - 2.3025851 * jax.random.uniform(keys[1], (NR, NA), jnp.float32) ** steps_of(keys[1], (NR, NA), ((0, 12), (1, 64)), -0.2, 0.2)), 0.05, 0.5)
    rotation = jnp.clip(jnp.exp(jax.random.uniform(keys[2], (NR,), jnp.float32, math.log(0.2), math.log(2.0))), 0.2, 2.0)
    shift_blocks = place_ends(jax.random.randint(keys[3], (STEPS, NR), 0, NB), jax.random.fold_in(keys[3], 1), 0, NB - 1).astype(jnp.int32)
    return {"fields": fields, "viscosity": viscosity, "rotation": rotation, "shift_blocks": shift_blocks}


time_step = 0.3


def rates(ext, viscosity, rotation):
    centre = ext[:, :, 1:-1, 1:-1]
    north = ext[:, :, 2:, 1:-1]
    south = ext[:, :, :-2, 1:-1]
    ahead = ext[:, :, 1:-1, 2:]
    behind = ext[:, :, 1:-1, :-2]
    above = jnp.concatenate([centre[:, 1:], centre[:, -1:]], axis=1)
    below = jnp.concatenate([centre[:, :1], centre[:, :-1]], axis=1)
    spread = viscosity * (north + south + ahead + behind + above + below - 6.0 * centre)
    radial_grad = 0.5 * (north - south)
    azimuth_grad = 0.5 * (ahead - behind)
    spin = rotation[:, None]
    rate_density = spread[0] - radial_grad[1] - azimuth_grad[2]
    rate_radial = spread[1] - radial_grad[0] + 2.0 * spin * centre[2]
    rate_azimuth = spread[2] - azimuth_grad[0] - 0.5 * spin * centre[1]
    return jnp.stack([rate_density, rate_radial, rate_azimuth])


def extend(state):
    padded = jnp.pad(state, ((0, 0), (0, 0), (1, 1), (0, 0)))
    return jnp.concatenate([padded[..., -1:], padded, padded[..., :1]], axis=3)


def advect(state, shifts):
    total = state.shape[3]
    count = total // BLOCK
    blocks = state.reshape(3, state.shape[1], state.shape[2], count, BLOCK)
    index = (lax.iota(jnp.int32, count)[None, :] - shifts.astype(jnp.int32)[:, None]) % count
    index = jnp.broadcast_to(index[None, None, :, :, None], blocks.shape).astype(jnp.int32)
    moved = jnp.take_along_axis(blocks, index, axis=3)
    return moved.reshape(state.shape)


def reference(fields, viscosity, rotation, shift_blocks):
    state = fields
    for step in range(STEPS):
        first = state + time_step * rates(extend(state), viscosity, rotation)
        second = 0.75 * state + 0.25 * (first + time_step * rates(extend(first), viscosity, rotation))
        state = state / 3.0 + (2.0 / 3.0) * (second + time_step * rates(extend(second), viscosity, rotation))
        state = advect(state, shift_blocks[step])
    return state
```

```python
import jax
import jax.numpy as jnp
from jax import lax
from jax.sharding import PartitionSpec as P

BLOCK = 64
HALO = 3


time_step = 0.3


def exchange_halo(cells, width):
    n_r = lax.axis_size("rad")
    n_a = lax.axis_size("azi")
    both = ("rad", "azi")

    def lin(r, a):
        return r * n_a + a

    up = [(i, i + 1) for i in range(n_r - 1)]
    down = [(i + 1, i) for i in range(n_r - 1)]
    fwd = [(i, (i + 1) % n_a) for i in range(n_a)]
    back = [((i + 1) % n_a, i) for i in range(n_a)]

    def diag(pairs_r, pairs_a):
        return [(lin(r0, a0), lin(r1, a1)) for r0, r1 in pairs_r for a0, a1 in pairs_a]

    top = cells[:, :width, :]
    bottom = cells[:, -width:, :]
    south = lax.ppermute(bottom, "rad", up)
    north = lax.ppermute(top, "rad", down)
    behind = lax.ppermute(cells[:, :, -width:], "azi", fwd)
    ahead = lax.ppermute(cells[:, :, :width], "azi", back)
    south_behind = lax.ppermute(bottom[:, :, -width:], both, diag(up, fwd))
    south_ahead = lax.ppermute(bottom[:, :, :width], both, diag(up, back))
    north_behind = lax.ppermute(top[:, :, -width:], both, diag(down, fwd))
    north_ahead = lax.ppermute(top[:, :, :width], both, diag(down, back))
    rows_south = jnp.concatenate([south_behind, south, south_ahead], axis=2)
    rows_mid = jnp.concatenate([behind, cells, ahead], axis=2)
    rows_north = jnp.concatenate([north_behind, north, north_ahead], axis=2)
    return jnp.concatenate([rows_south, rows_mid, rows_north], axis=1)


def rates(state, viscosity, spin):
    centre = state[:, :, 1:-1, 1:-1]
    north = state[:, :, 2:, 1:-1]
    south = state[:, :, :-2, 1:-1]
    ahead = state[:, :, 1:-1, 2:]
    behind = state[:, :, 1:-1, :-2]
    above = jnp.concatenate([centre[:, 1:], centre[:, -1:]], axis=1)
    below = jnp.concatenate([centre[:, :1], centre[:, :-1]], axis=1)
    spread = viscosity * (north + south + ahead + behind + above + below - 6.0 * centre)
    radial_grad = 0.5 * (north - south)
    azimuth_grad = 0.5 * (ahead - behind)
    rate_density = spread[0] - radial_grad[1] - azimuth_grad[2]
    rate_radial = spread[1] - radial_grad[0] + 2.0 * spin * centre[2]
    rate_azimuth = spread[2] - azimuth_grad[0] - 0.5 * spin * centre[1]
    return jnp.stack([rate_density, rate_radial, rate_azimuth])


def advect(state, shift_row, first_row):
    fields, heights, radii, cells = state.shape
    lines = jnp.swapaxes(state.reshape(fields, heights * radii, cells), 0, 1)
    ring = lax.all_to_all(lines, "azi", 0, 0, tiled=True)
    chunks = ring.shape[0]
    me = lax.axis_index("azi")
    shift = lax.dynamic_index_in_dim(shift_row, first_row + me % radii, keepdims=False)
    per_chunk = cells // BLOCK
    count = chunks * per_chunk
    shift = shift % count
    whole = shift // per_chunk
    part = shift % per_chunk
    doubled = jnp.concatenate([ring, ring], axis=0)
    lane = lax.broadcasted_iota(jnp.int32, ring.shape, 2)
    base = lax.dynamic_slice_in_dim(doubled, (chunks - whole) % chunks, chunks, 0)
    earlier = lax.dynamic_slice_in_dim(doubled, (chunks - whole - 1) % chunks, chunks, 0)
    rolled = base
    for step in range(1, per_chunk):
        mixed = jnp.roll(jnp.where(lane < cells - step * BLOCK, base, earlier), step * BLOCK, axis=2)
        rolled = jnp.where(part == step, mixed, rolled)
    back = lax.all_to_all(rolled, "azi", 0, 0, tiled=True)
    return jnp.swapaxes(back, 0, 1).reshape(fields, heights, radii, cells)


def body(fields, viscosity, rotation, shift_blocks):
    n_f, heights, radii, cells = fields.shape
    w = HALO
    band = lax.axis_index("rad")
    first_row = band * radii
    total_rows = rotation.shape[0]
    packed = jnp.concatenate([fields.reshape(n_f * heights, radii, cells), viscosity[None]], axis=0)
    ext = exchange_halo(packed, w)
    u0 = ext[: n_f * heights].reshape(n_f, heights, radii + 2 * w, cells + 2 * w)
    visc = ext[n_f * heights]
    rot = jnp.concatenate([jnp.zeros((w,), rotation.dtype), rotation, jnp.zeros((w,), rotation.dtype)])
    spin = lax.dynamic_slice_in_dim(rot, first_row, radii + 2 * w)[:, None]
    row = first_row - w + lax.iota(jnp.int32, radii + 2 * w)
    inside = ((row >= 0) & (row < total_rows))[:, None]

    def trim(x, k):
        return x[..., k : x.shape[-2] - k, k : x.shape[-1] - k]

    def rates_at(state, k):
        return rates(state, trim(visc, k), spin[k : spin.shape[0] - k])

    def keep(state, k):
        return jnp.where(inside[k : inside.shape[0] - k], state, 0.0)

    state = u0
    first = keep(trim(state, 1) + time_step * rates_at(state, 1), 1)
    second = keep(0.75 * trim(state, 2) + 0.25 * (trim(first, 1) + time_step * rates_at(first, 2)), 2)
    state = trim(state, 3) / 3.0 + 2.0 / 3.0 * (trim(second, 1) + time_step * rates_at(second, 3))
    for t in range(shift_blocks.shape[0]):
        state = advect(state, shift_blocks[t], first_row)
    return state


def solution(mesh):
    return jax.shard_map(
        body,
        mesh=mesh,
        in_specs=(P(None, None, "rad", "azi"), P("rad", "azi"), P(), P()),
        out_specs=P(None, None, "rad", "azi"),
        check_vma=False,
    )
```

```python
import jax
import jax.numpy as jnp
from jax import lax
from jax.sharding import PartitionSpec as P

BLOCK = 64
HALO = 3


time_step = 0.3


def exchange_halo(cells, width):
    n_r = lax.axis_size("rad")
    n_a = lax.axis_size("azi")
    up = [(i, i + 1) for i in range(n_r - 1)]
    down = [(i + 1, i) for i in range(n_r - 1)]
    fwd = [(i, (i + 1) % n_a) for i in range(n_a)]
    back = [((i + 1) % n_a, i) for i in range(n_a)]
    behind = lax.ppermute(cells[:, :, -width:], "azi", fwd)
    ahead = lax.ppermute(cells[:, :, :width], "azi", back)
    wide = jnp.concatenate([behind, cells, ahead], axis=2)
    south = lax.ppermute(wide[:, -width:, :], "rad", up)
    north = lax.ppermute(wide[:, :width, :], "rad", down)
    return jnp.concatenate([south, wide, north], axis=1)


def rates(state, viscosity, spin):
    centre = state[:, :, 1:-1, 1:-1]
    north = state[:, :, 2:, 1:-1]
    south = state[:, :, :-2, 1:-1]
    ahead = state[:, :, 1:-1, 2:]
    behind = state[:, :, 1:-1, :-2]
    above = jnp.concatenate([centre[:, 1:], centre[:, -1:]], axis=1)
    below = jnp.concatenate([centre[:, :1], centre[:, :-1]], axis=1)
    spread = viscosity * (north + south + ahead + behind + above + below - 6.0 * centre)
    radial_grad = 0.5 * (north - south)
    azimuth_grad = 0.5 * (ahead - behind)
    rate_density = spread[0] - radial_grad[1] - azimuth_grad[2]
    rate_radial = spread[1] - radial_grad[0] + 2.0 * spin * centre[2]
    rate_azimuth = spread[2] - azimuth_grad[0] - 0.5 * spin * centre[1]
    return jnp.stack([rate_density, rate_radial, rate_azimuth])


def advect(state, shift_row, first_row):
    fields, heights, radii, cells = state.shape
    lines = jnp.swapaxes(state.reshape(fields, heights * radii, cells), 0, 1)
    ring = lax.all_to_all(lines, "azi", 0, 0, tiled=True)
    chunks = ring.shape[0]
    me = lax.axis_index("azi")
    shift = lax.dynamic_index_in_dim(shift_row, first_row + me % radii, keepdims=False)
    per_chunk = cells // BLOCK
    count = chunks * per_chunk
    shift = shift % count
    whole = shift // per_chunk
    part = shift % per_chunk
    doubled = jnp.concatenate([ring, ring], axis=0)
    lane = lax.broadcasted_iota(jnp.int32, ring.shape, 2)
    base = lax.dynamic_slice_in_dim(doubled, (chunks - whole) % chunks, chunks, 0)
    earlier = lax.dynamic_slice_in_dim(doubled, (chunks - whole - 1) % chunks, chunks, 0)
    rolled = base
    for step in range(1, per_chunk):
        mixed = jnp.roll(jnp.where(lane < cells - step * BLOCK, base, earlier), step * BLOCK, axis=2)
        rolled = jnp.where(part == step, mixed, rolled)
    back = lax.all_to_all(rolled, "azi", 0, 0, tiled=True)
    return jnp.swapaxes(back, 0, 1).reshape(fields, heights, radii, cells)


def body(fields, viscosity, rotation, shift_blocks):
    n_f, heights, radii, cells = fields.shape
    w = HALO
    band = lax.axis_index("rad")
    first_row = band * radii
    total_rows = rotation.shape[0]
    packed = jnp.concatenate([fields.reshape(n_f * heights, radii, cells), viscosity[None]], axis=0)
    ext = exchange_halo(packed, w)
    u0 = ext[: n_f * heights].reshape(n_f, heights, radii + 2 * w, cells + 2 * w)
    visc = ext[n_f * heights]
    rot = jnp.concatenate([jnp.zeros((w,), rotation.dtype), rotation, jnp.zeros((w,), rotation.dtype)])
    spin = lax.dynamic_slice_in_dim(rot, first_row, radii + 2 * w)[:, None]
    row = first_row - w + lax.iota(jnp.int32, radii + 2 * w)
    inside = ((row >= 0) & (row < total_rows))[:, None]

    def trim(x, k):
        return x[..., k : x.shape[-2] - k, k : x.shape[-1] - k]

    def rates_at(state, k):
        return rates(state, trim(visc, k), spin[k : spin.shape[0] - k])

    def keep(state, k):
        return jnp.where(inside[k : inside.shape[0] - k], state, 0.0)

    state = u0
    first = keep(trim(state, 1) + time_step * rates_at(state, 1), 1)
    second = keep(0.75 * trim(state, 2) + 0.25 * (trim(first, 1) + time_step * rates_at(first, 2)), 2)
    state = trim(state, 3) / 3.0 + 2.0 / 3.0 * (trim(second, 1) + time_step * rates_at(second, 3))
    for t in range(shift_blocks.shape[0]):
        state = advect(state, shift_blocks[t], first_row)
    return state


def solution(mesh):
    return jax.shard_map(
        body,
        mesh=mesh,
        in_specs=(P(None, None, "rad", "azi"), P("rad", "azi"), P(), P()),
        out_specs=P(None, None, "rad", "azi"),
        check_vma=False,
    )
```

```python
import jax
import jax.numpy as jnp
from jax import lax
from jax.sharding import PartitionSpec as P

BLOCK = 64
HALO = 3


time_step = 0.3


def exchange_halo(cells, width):
    n_r = lax.axis_size("rad")
    n_a = lax.axis_size("azi")
    up = [(i, i + 1) for i in range(n_r - 1)]
    down = [(i + 1, i) for i in range(n_r - 1)]
    fwd = [(i, (i + 1) % n_a) for i in range(n_a)]
    back = [((i + 1) % n_a, i) for i in range(n_a)]
    behind = lax.ppermute(cells[:, :, -width:], "azi", fwd)
    ahead = lax.ppermute(cells[:, :, :width], "azi", back)
    wide = jnp.concatenate([behind, cells, ahead], axis=2)
    south = lax.ppermute(wide[:, -width:, :], "rad", up)
    north = lax.ppermute(wide[:, :width, :], "rad", down)
    return jnp.concatenate([south, wide, north], axis=1)


def rates(state, viscosity, spin):
    centre = state[:, :, 1:-1, 1:-1]
    north = state[:, :, 2:, 1:-1]
    south = state[:, :, :-2, 1:-1]
    ahead = state[:, :, 1:-1, 2:]
    behind = state[:, :, 1:-1, :-2]
    above = jnp.concatenate([centre[:, 1:], centre[:, -1:]], axis=1)
    below = jnp.concatenate([centre[:, :1], centre[:, :-1]], axis=1)
    spread = viscosity * (north + south + ahead + behind + above + below - 6.0 * centre)
    radial_grad = 0.5 * (north - south)
    azimuth_grad = 0.5 * (ahead - behind)
    rate_density = spread[0] - radial_grad[1] - azimuth_grad[2]
    rate_radial = spread[1] - radial_grad[0] + 2.0 * spin * centre[2]
    rate_azimuth = spread[2] - azimuth_grad[0] - 0.5 * spin * centre[1]
    return jnp.stack([rate_density, rate_radial, rate_azimuth])


def exchange_rows(cells, width):
    n_r = lax.axis_size("rad")
    up = [(i, i + 1) for i in range(n_r - 1)]
    down = [(i + 1, i) for i in range(n_r - 1)]
    south = lax.ppermute(cells[:, -width:], "rad", up)
    north = lax.ppermute(cells[:, :width], "rad", down)
    return jnp.concatenate([south, cells, north], axis=1)


def rates_ring(state, viscosity, spin):
    centre = state[:, :, 1:-1]
    north = state[:, :, 2:]
    south = state[:, :, :-2]
    ahead = jnp.roll(centre, -1, axis=-1)
    behind = jnp.roll(centre, 1, axis=-1)
    above = jnp.concatenate([centre[:, 1:], centre[:, -1:]], axis=1)
    below = jnp.concatenate([centre[:, :1], centre[:, :-1]], axis=1)
    spread = viscosity * (north + south + ahead + behind + above + below - 6.0 * centre)
    radial_grad = 0.5 * (north - south)
    azimuth_grad = 0.5 * (ahead - behind)
    rate_density = spread[0] - radial_grad[1] - azimuth_grad[2]
    rate_radial = spread[1] - radial_grad[0] + 2.0 * spin * centre[2]
    rate_azimuth = spread[2] - azimuth_grad[0] - 0.5 * spin * centre[1]
    return jnp.stack([rate_density, rate_radial, rate_azimuth])


def runge_kutta(u0, rates_at, keep, trim):
    first = keep(trim(u0, 1) + time_step * rates_at(u0, 1), 1)
    second = keep(0.75 * trim(u0, 2) + 0.25 * (trim(first, 1) + time_step * rates_at(first, 2)), 2)
    return trim(u0, 3) / 3.0 + 2.0 / 3.0 * (trim(second, 1) + time_step * rates_at(second, 3))


def body(fields, viscosity, rotation, shift_blocks):
    n_f, heights, radii, cells = fields.shape
    w = HALO
    edge = 2 * w
    band = lax.axis_index("rad")
    first_row = band * radii
    total_rows = rotation.shape[0]
    planes = n_f * heights
    packed = jnp.concatenate([fields.reshape(planes, radii, cells), viscosity[None]], axis=0)
    rows = exchange_rows(packed, w)
    rot = jnp.concatenate([jnp.zeros((w,), rotation.dtype), rotation, jnp.zeros((w,), rotation.dtype)])

    ext = jnp.pad(rows, ((0, 0), (0, 0), (w, w)))
    u0 = ext[:planes].reshape(n_f, heights, radii + 2 * w, cells + 2 * w)
    visc = ext[planes]
    spin = lax.dynamic_slice_in_dim(rot, first_row, radii + 2 * w)[:, None]
    row = first_row - w + lax.iota(jnp.int32, radii + 2 * w)
    inside = ((row >= 0) & (row < total_rows))[:, None]

    def trim(x, k):
        return x[..., k : x.shape[-2] - k, k : x.shape[-1] - k]

    def rates_at(state, k):
        return rates(state, trim(visc, k), spin[k : spin.shape[0] - k])

    def keep(state, k):
        return jnp.where(inside[k : inside.shape[0] - k], state, 0.0)

    state = runge_kutta(u0, rates_at, keep, trim)

    lines = jnp.swapaxes(state.reshape(n_f, heights * radii, cells), 0, 1)
    chunks = lines.shape[0]
    edges = jnp.concatenate([rows[:, :, :edge], rows[:, :, cells - edge :]], axis=2)
    wins = jnp.stack([edges[:, r : r + 2 * w + 1] for r in range(radii)])
    win_size = wins[0].size
    win_rows = -(-win_size // cells)
    wins = jnp.pad(wins.reshape(radii, win_size), ((0, 0), (0, win_rows * cells - win_size)))
    wins = jnp.tile(wins.reshape(radii, win_rows, cells), (chunks // radii, 1, 1))
    ring = lax.all_to_all(jnp.concatenate([lines, wins], axis=1), "azi", 0, 0, tiled=True)
    line = ring[:, :n_f]
    raw = ring[:, n_f:].reshape(chunks, win_rows * cells)[:, :win_size]
    raw = raw.reshape(chunks, planes + 1, 2 * w + 1, 2 * edge)

    me = lax.axis_index("azi")
    my_h = me // radii
    my_r = me % radii
    window = jnp.concatenate([jnp.roll(raw, 1, axis=0)[..., edge:], raw[..., :edge]], axis=-1)
    window = jnp.transpose(window, (1, 2, 0, 3)).reshape(planes + 1, 2 * w + 1, chunks * 2 * edge)
    b0 = window[:planes].reshape(n_f, heights, 2 * w + 1, chunks * 2 * edge)
    b_visc = window[planes]
    b_spin = lax.dynamic_slice_in_dim(rot, first_row + my_r, 2 * w + 1)[:, None]
    b_row = first_row + my_r - w + lax.iota(jnp.int32, 2 * w + 1)
    b_inside = ((b_row >= 0) & (b_row < total_rows))[:, None]

    def b_trim(x, k):
        return x[..., k : x.shape[-2] - k, :]

    def b_rates_at(state, k):
        return rates_ring(state, b_visc[k : b_visc.shape[0] - k], b_spin[k : b_spin.shape[0] - k])

    def b_keep(state, k):
        return jnp.where(b_inside[k : b_inside.shape[0] - k], state, 0.0)

    fixed = runge_kutta(b0, b_rates_at, b_keep, b_trim)[:, :, 0]
    fixed = lax.dynamic_index_in_dim(fixed, my_h, axis=1, keepdims=False)
    fixed = jnp.swapaxes(fixed.reshape(n_f, chunks, 2 * edge), 0, 1)
    line = jnp.concatenate(
        [fixed[:, :, edge : edge + w], line[:, :, w : cells - w], jnp.roll(fixed, -1, axis=0)[:, :, edge - w : edge]],
        axis=2,
    )

    for t in range(shift_blocks.shape[0]):
        shift = lax.dynamic_index_in_dim(shift_blocks[t], first_row + my_r, keepdims=False)
        per_chunk = cells // BLOCK
        count = chunks * per_chunk
        shift = shift % count
        whole = shift // per_chunk
        part = shift % per_chunk
        doubled = jnp.concatenate([line, line], axis=0)
        lane = lax.broadcasted_iota(jnp.int32, line.shape, 2)
        base = lax.dynamic_slice_in_dim(doubled, (chunks - whole) % chunks, chunks, 0)
        earlier = lax.dynamic_slice_in_dim(doubled, (chunks - whole - 1) % chunks, chunks, 0)
        rolled = base
        for step in range(1, per_chunk):
            mixed = jnp.roll(jnp.where(lane < cells - step * BLOCK, base, earlier), step * BLOCK, axis=2)
            rolled = jnp.where(part == step, mixed, rolled)
        line = rolled
    back = lax.all_to_all(line, "azi", 0, 0, tiled=True)
    return jnp.swapaxes(back, 0, 1).reshape(n_f, heights, radii, cells)


def solution(mesh):
    return jax.shard_map(
        body,
        mesh=mesh,
        in_specs=(P(None, None, "rad", "azi"), P("rad", "azi"), P(), P()),
        out_specs=P(None, None, "rad", "azi"),
        check_vma=False,
    )
```

```python
import jax
import jax.numpy as jnp
from jax import lax
from jax.sharding import PartitionSpec as P

BLOCK = 64
HALO = 3


time_step = 0.3


def exchange_halo(cells, width):
    n_r = lax.axis_size("rad")
    n_a = lax.axis_size("azi")
    up = [(i, i + 1) for i in range(n_r - 1)]
    down = [(i + 1, i) for i in range(n_r - 1)]
    fwd = [(i, (i + 1) % n_a) for i in range(n_a)]
    behind = lax.ppermute(cells[:, :, cells.shape[2] - 2 * width :], "azi", fwd)
    wide = jnp.concatenate([behind, cells], axis=2)
    south = lax.ppermute(wide[:, -width:, :], "rad", up)
    north = lax.ppermute(wide[:, :width, :], "rad", down)
    return jnp.concatenate([south, wide, north], axis=1)


def rates(state, viscosity, spin):
    centre = state[:, :, 1:-1, 1:-1]
    north = state[:, :, 2:, 1:-1]
    south = state[:, :, :-2, 1:-1]
    ahead = state[:, :, 1:-1, 2:]
    behind = state[:, :, 1:-1, :-2]
    above = jnp.concatenate([centre[:, 1:], centre[:, -1:]], axis=1)
    below = jnp.concatenate([centre[:, :1], centre[:, :-1]], axis=1)
    spread = viscosity * (north + south + ahead + behind + above + below - 6.0 * centre)
    radial_grad = 0.5 * (north - south)
    azimuth_grad = 0.5 * (ahead - behind)
    rate_density = spread[0] - radial_grad[1] - azimuth_grad[2]
    rate_radial = spread[1] - radial_grad[0] + 2.0 * spin * centre[2]
    rate_azimuth = spread[2] - azimuth_grad[0] - 0.5 * spin * centre[1]
    return jnp.stack([rate_density, rate_radial, rate_azimuth])


def advect(state, shift_row, first_row, lag):
    fields, heights, radii, cells = state.shape
    lines = jnp.swapaxes(state.reshape(fields, heights * radii, cells), 0, 1)
    ring = lax.all_to_all(lines, "azi", 0, 0, tiled=True)
    ring = jnp.concatenate([ring[:, :, lag:], jnp.roll(ring, -1, axis=0)[:, :, :lag]], axis=2)
    chunks = ring.shape[0]
    me = lax.axis_index("azi")
    shift = lax.dynamic_index_in_dim(shift_row, first_row + me % radii, keepdims=False)
    per_chunk = cells // BLOCK
    count = chunks * per_chunk
    shift = shift % count
    whole = shift // per_chunk
    part = shift % per_chunk
    doubled = jnp.concatenate([ring, ring], axis=0)
    lane = lax.broadcasted_iota(jnp.int32, ring.shape, 2)
    base = lax.dynamic_slice_in_dim(doubled, (chunks - whole) % chunks, chunks, 0)
    earlier = lax.dynamic_slice_in_dim(doubled, (chunks - whole - 1) % chunks, chunks, 0)
    rolled = base
    for step in range(1, per_chunk):
        mixed = jnp.roll(jnp.where(lane < cells - step * BLOCK, base, earlier), step * BLOCK, axis=2)
        rolled = jnp.where(part == step, mixed, rolled)
    back = lax.all_to_all(rolled, "azi", 0, 0, tiled=True)
    return jnp.swapaxes(back, 0, 1).reshape(fields, heights, radii, cells)


def body(fields, viscosity, rotation, shift_blocks):
    n_f, heights, radii, cells = fields.shape
    w = HALO
    band = lax.axis_index("rad")
    first_row = band * radii
    total_rows = rotation.shape[0]
    packed = jnp.concatenate([fields.reshape(n_f * heights, radii, cells), viscosity[None]], axis=0)
    ext = exchange_halo(packed, w)
    u0 = ext[: n_f * heights].reshape(n_f, heights, radii + 2 * w, cells + 2 * w)
    visc = ext[n_f * heights]
    rot = jnp.concatenate([jnp.zeros((w,), rotation.dtype), rotation, jnp.zeros((w,), rotation.dtype)])
    spin = lax.dynamic_slice_in_dim(rot, first_row, radii + 2 * w)[:, None]
    row = first_row - w + lax.iota(jnp.int32, radii + 2 * w)
    inside = ((row >= 0) & (row < total_rows))[:, None]

    def trim(x, k):
        return x[..., k : x.shape[-2] - k, k : x.shape[-1] - k]

    def rates_at(state, k):
        return rates(state, trim(visc, k), spin[k : spin.shape[0] - k])

    def keep(state, k):
        return jnp.where(inside[k : inside.shape[0] - k], state, 0.0)

    state = u0
    first = keep(trim(state, 1) + time_step * rates_at(state, 1), 1)
    second = keep(0.75 * trim(state, 2) + 0.25 * (trim(first, 1) + time_step * rates_at(first, 2)), 2)
    state = trim(state, 3) / 3.0 + 2.0 / 3.0 * (trim(second, 1) + time_step * rates_at(second, 3))
    for t in range(shift_blocks.shape[0]):
        state = advect(state, shift_blocks[t], first_row, w)
    return state


def solution(mesh):
    return jax.shard_map(
        body,
        mesh=mesh,
        in_specs=(P(None, None, "rad", "azi"), P("rad", "azi"), P(), P()),
        out_specs=P(None, None, "rad", "azi"),
        check_vma=False,
    )
```

```python
import jax
import jax.numpy as jnp
from jax import lax
from jax.sharding import PartitionSpec as P

BLOCK = 64
HALO = 3


time_step = 0.3


def exchange_halo(cells, width):
    n_r = lax.axis_size("rad")
    n_a = lax.axis_size("azi")
    up = [(i, i + 1) for i in range(n_r - 1)]
    down = [(i + 1, i) for i in range(n_r - 1)]
    fwd = [(i, (i + 1) % n_a) for i in range(n_a)]

    def diag(pairs_r):
        return [(r0 * n_a + a0, r1 * n_a + a1) for r0, r1 in pairs_r for a0, a1 in fwd]

    tail = cells[:, :, cells.shape[2] - 2 * width :]
    behind = lax.ppermute(tail, "azi", fwd)
    south_behind = lax.ppermute(tail[:, -width:], ("rad", "azi"), diag(up))
    north_behind = lax.ppermute(tail[:, :width], ("rad", "azi"), diag(down))
    south = lax.ppermute(cells[:, -width:], "rad", up)
    north = lax.ppermute(cells[:, :width], "rad", down)
    return jnp.concatenate(
        [
            jnp.concatenate([south_behind, south], axis=2),
            jnp.concatenate([behind, cells], axis=2),
            jnp.concatenate([north_behind, north], axis=2),
        ],
        axis=1,
    )


def rates(state, viscosity, spin):
    centre = state[:, :, 1:-1, 1:-1]
    north = state[:, :, 2:, 1:-1]
    south = state[:, :, :-2, 1:-1]
    ahead = state[:, :, 1:-1, 2:]
    behind = state[:, :, 1:-1, :-2]
    above = jnp.concatenate([centre[:, 1:], centre[:, -1:]], axis=1)
    below = jnp.concatenate([centre[:, :1], centre[:, :-1]], axis=1)
    spread = viscosity * (north + south + ahead + behind + above + below - 6.0 * centre)
    radial_grad = 0.5 * (north - south)
    azimuth_grad = 0.5 * (ahead - behind)
    rate_density = spread[0] - radial_grad[1] - azimuth_grad[2]
    rate_radial = spread[1] - radial_grad[0] + 2.0 * spin * centre[2]
    rate_azimuth = spread[2] - azimuth_grad[0] - 0.5 * spin * centre[1]
    return jnp.stack([rate_density, rate_radial, rate_azimuth])


def advect(state, shift_row, first_row, lag):
    fields, heights, radii, cells = state.shape
    lines = jnp.swapaxes(state.reshape(fields, heights * radii, cells), 0, 1)
    ring = lax.all_to_all(lines, "azi", 0, 0, tiled=True)
    ring = jnp.concatenate([ring[:, :, lag:], jnp.roll(ring, -1, axis=0)[:, :, :lag]], axis=2)
    chunks = ring.shape[0]
    me = lax.axis_index("azi")
    shift = lax.dynamic_index_in_dim(shift_row, first_row + me % radii, keepdims=False)
    per_chunk = cells // BLOCK
    count = chunks * per_chunk
    shift = shift % count
    whole = shift // per_chunk
    part = shift % per_chunk
    doubled = jnp.concatenate([ring, ring], axis=0)
    lane = lax.broadcasted_iota(jnp.int32, ring.shape, 2)
    base = lax.dynamic_slice_in_dim(doubled, (chunks - whole) % chunks, chunks, 0)
    earlier = lax.dynamic_slice_in_dim(doubled, (chunks - whole - 1) % chunks, chunks, 0)
    rolled = base
    for step in range(1, per_chunk):
        mixed = jnp.roll(jnp.where(lane < cells - step * BLOCK, base, earlier), step * BLOCK, axis=2)
        rolled = jnp.where(part == step, mixed, rolled)
    back = lax.all_to_all(rolled, "azi", 0, 0, tiled=True)
    return jnp.swapaxes(back, 0, 1).reshape(fields, heights, radii, cells)


def body(fields, viscosity, rotation, shift_blocks):
    n_f, heights, radii, cells = fields.shape
    w = HALO
    band = lax.axis_index("rad")
    first_row = band * radii
    total_rows = rotation.shape[0]
    packed = jnp.concatenate([fields.reshape(n_f * heights, radii, cells), viscosity[None]], axis=0)
    ext = exchange_halo(packed, w)
    u0 = ext[: n_f * heights].reshape(n_f, heights, radii + 2 * w, cells + 2 * w)
    visc = ext[n_f * heights]
    rot = jnp.concatenate([jnp.zeros((w,), rotation.dtype), rotation, jnp.zeros((w,), rotation.dtype)])
    spin = lax.dynamic_slice_in_dim(rot, first_row, radii + 2 * w)[:, None]
    row = first_row - w + lax.iota(jnp.int32, radii + 2 * w)
    inside = ((row >= 0) & (row < total_rows))[:, None]

    def trim(x, k):
        return x[..., k : x.shape[-2] - k, k : x.shape[-1] - k]

    def rates_at(state, k):
        return rates(state, trim(visc, k), spin[k : spin.shape[0] - k])

    def keep(state, k):
        return jnp.where(inside[k : inside.shape[0] - k], state, 0.0)

    state = u0
    first = keep(trim(state, 1) + time_step * rates_at(state, 1), 1)
    second = keep(0.75 * trim(state, 2) + 0.25 * (trim(first, 1) + time_step * rates_at(first, 2)), 2)
    state = trim(state, 3) / 3.0 + 2.0 / 3.0 * (trim(second, 1) + time_step * rates_at(second, 3))
    for t in range(shift_blocks.shape[0]):
        state = advect(state, shift_blocks[t], first_row, w)
    return state


def solution(mesh):
    return jax.shard_map(
        body,
        mesh=mesh,
        in_specs=(P(None, None, "rad", "azi"), P("rad", "azi"), P(), P()),
        out_specs=P(None, None, "rad", "azi"),
        check_vma=False,
    )
```

```python
import jax
import jax.numpy as jnp
from jax import lax
from jax.sharding import PartitionSpec as P

BLOCK = 64
HALO = 3


time_step = 0.3


def rates(state, viscosity, spin):
    centre = state[:, :, 1:-1, 1:-1]
    north = state[:, :, 2:, 1:-1]
    south = state[:, :, :-2, 1:-1]
    ahead = state[:, :, 1:-1, 2:]
    behind = state[:, :, 1:-1, :-2]
    above = jnp.concatenate([centre[:, 1:], centre[:, -1:]], axis=1)
    below = jnp.concatenate([centre[:, :1], centre[:, :-1]], axis=1)
    spread = viscosity * (north + south + ahead + behind + above + below - 6.0 * centre)
    radial_grad = 0.5 * (north - south)
    azimuth_grad = 0.5 * (ahead - behind)
    rate_density = spread[0] - radial_grad[1] - azimuth_grad[2]
    rate_radial = spread[1] - radial_grad[0] + 2.0 * spin * centre[2]
    rate_azimuth = spread[2] - azimuth_grad[0] - 0.5 * spin * centre[1]
    return jnp.stack([rate_density, rate_radial, rate_azimuth])


def advect(state, shift_row, first_row, lag):
    fields, heights, radii, cells = state.shape
    lines = jnp.swapaxes(state.reshape(fields, heights * radii, cells), 0, 1)
    ring = lax.all_to_all(lines, "azi", 0, 0, tiled=True)
    ring = jnp.concatenate([ring[:, :, lag:], jnp.roll(ring, -1, axis=0)[:, :, :lag]], axis=2)
    chunks = ring.shape[0]
    me = lax.axis_index("azi")
    shift = lax.dynamic_index_in_dim(shift_row, first_row + me % radii, keepdims=False)
    per_chunk = cells // BLOCK
    count = chunks * per_chunk
    shift = shift % count
    whole = shift // per_chunk
    part = shift % per_chunk
    doubled = jnp.concatenate([ring, ring], axis=0)
    lane = lax.broadcasted_iota(jnp.int32, ring.shape, 2)
    base = lax.dynamic_slice_in_dim(doubled, (chunks - whole) % chunks, chunks, 0)
    earlier = lax.dynamic_slice_in_dim(doubled, (chunks - whole - 1) % chunks, chunks, 0)
    rolled = base
    for step in range(1, per_chunk):
        mixed = jnp.roll(jnp.where(lane < cells - step * BLOCK, base, earlier), step * BLOCK, axis=2)
        rolled = jnp.where(part == step, mixed, rolled)
    back = lax.all_to_all(rolled, "azi", 0, 0, tiled=True)
    return jnp.swapaxes(back, 0, 1).reshape(fields, heights, radii, cells)


def body(fields, viscosity, rotation, shift_blocks):
    n_f, heights, radii, cells = fields.shape
    w = HALO
    n_r = lax.axis_size("rad")
    n_a = lax.axis_size("azi")
    band = lax.axis_index("rad")
    first_row = band * radii
    total_rows = rotation.shape[0]
    planes = n_f * heights
    packed = jnp.concatenate([fields.reshape(planes, radii, cells), viscosity[None]], axis=0)

    up = [(i, i + 1) for i in range(n_r - 1)]
    down = [(i + 1, i) for i in range(n_r - 1)]
    south = lax.ppermute(packed[:, -w:], "rad", up)
    north = lax.ppermute(packed[:, :w], "rad", down)
    rows = jnp.concatenate([south, packed, north], axis=1)
    behind = lax.ppermute(rows[:, :, cells - 2 * w :], "azi", [(i, (i + 1) % n_a) for i in range(n_a)])

    rot = jnp.concatenate([jnp.zeros((w,), rotation.dtype), rotation, jnp.zeros((w,), rotation.dtype)])
    spin = lax.dynamic_slice_in_dim(rot, first_row, radii + 2 * w)[:, None]
    row = first_row - w + lax.iota(jnp.int32, radii + 2 * w)
    inside = ((row >= 0) & (row < total_rows))[:, None]

    def trim(x, k):
        return x[..., k : x.shape[-2] - k, k : x.shape[-1] - k]

    def runge_kutta(ext):
        u0 = ext[:planes].reshape(n_f, heights, radii + 2 * w, ext.shape[-1])
        visc = ext[planes]

        def rates_at(state, k):
            return rates(state, trim(visc, k), spin[k : spin.shape[0] - k])

        def keep(state, k):
            return jnp.where(inside[k : inside.shape[0] - k], state, 0.0)

        first = keep(trim(u0, 1) + time_step * rates_at(u0, 1), 1)
        second = keep(0.75 * trim(u0, 2) + 0.25 * (trim(first, 1) + time_step * rates_at(first, 2)), 2)
        return trim(u0, 3) / 3.0 + 2.0 / 3.0 * (trim(second, 1) + time_step * rates_at(second, 3))

    inner = runge_kutta(rows)
    edge = runge_kutta(jnp.concatenate([behind, rows[:, :, : 2 * w]], axis=2))
    state = jnp.concatenate([edge, inner], axis=-1)
    for t in range(shift_blocks.shape[0]):
        state = advect(state, shift_blocks[t], first_row, w)
    return state


def solution(mesh):
    return jax.shard_map(
        body,
        mesh=mesh,
        in_specs=(P(None, None, "rad", "azi"), P("rad", "azi"), P(), P()),
        out_specs=P(None, None, "rad", "azi"),
        check_vma=False,
    )
```

```python
import jax
import jax.numpy as jnp
from jax import lax
from jax.sharding import PartitionSpec as P

BLOCK = 64
HALO = 3


time_step = 0.3


def exchange_halo(cells, width):
    n_r = lax.axis_size("rad")
    n_a = lax.axis_size("azi")
    up = [(i, i + 1) for i in range(n_r - 1)]
    down = [(i + 1, i) for i in range(n_r - 1)]
    back = [((i + 1) % n_a, i) for i in range(n_a)]
    ahead = lax.ppermute(cells[:, :, : 2 * width], "azi", back)
    wide = jnp.concatenate([cells, ahead], axis=2)
    south = lax.ppermute(wide[:, -width:, :], "rad", up)
    north = lax.ppermute(wide[:, :width, :], "rad", down)
    return jnp.concatenate([south, wide, north], axis=1)


def rates(state, viscosity, spin):
    centre = state[:, :, 1:-1, 1:-1]
    north = state[:, :, 2:, 1:-1]
    south = state[:, :, :-2, 1:-1]
    ahead = state[:, :, 1:-1, 2:]
    behind = state[:, :, 1:-1, :-2]
    above = jnp.concatenate([centre[:, 1:], centre[:, -1:]], axis=1)
    below = jnp.concatenate([centre[:, :1], centre[:, :-1]], axis=1)
    spread = viscosity * (north + south + ahead + behind + above + below - 6.0 * centre)
    radial_grad = 0.5 * (north - south)
    azimuth_grad = 0.5 * (ahead - behind)
    rate_density = spread[0] - radial_grad[1] - azimuth_grad[2]
    rate_radial = spread[1] - radial_grad[0] + 2.0 * spin * centre[2]
    rate_azimuth = spread[2] - azimuth_grad[0] - 0.5 * spin * centre[1]
    return jnp.stack([rate_density, rate_radial, rate_azimuth])


def advect(state, shift_row, first_row, lag):
    fields, heights, radii, cells = state.shape
    lines = jnp.swapaxes(state.reshape(fields, heights * radii, cells), 0, 1)
    ring = lax.all_to_all(lines, "azi", 0, 0, tiled=True)
    ring = jnp.concatenate([jnp.roll(ring, 1, axis=0)[:, :, cells - lag :], ring[:, :, : cells - lag]], axis=2)
    chunks = ring.shape[0]
    me = lax.axis_index("azi")
    shift = lax.dynamic_index_in_dim(shift_row, first_row + me % radii, keepdims=False)
    per_chunk = cells // BLOCK
    count = chunks * per_chunk
    shift = shift % count
    whole = shift // per_chunk
    part = shift % per_chunk
    doubled = jnp.concatenate([ring, ring], axis=0)
    lane = lax.broadcasted_iota(jnp.int32, ring.shape, 2)
    base = lax.dynamic_slice_in_dim(doubled, (chunks - whole) % chunks, chunks, 0)
    earlier = lax.dynamic_slice_in_dim(doubled, (chunks - whole - 1) % chunks, chunks, 0)
    rolled = base
    for step in range(1, per_chunk):
        mixed = jnp.roll(jnp.where(lane < cells - step * BLOCK, base, earlier), step * BLOCK, axis=2)
        rolled = jnp.where(part == step, mixed, rolled)
    back = lax.all_to_all(rolled, "azi", 0, 0, tiled=True)
    return jnp.swapaxes(back, 0, 1).reshape(fields, heights, radii, cells)


def body(fields, viscosity, rotation, shift_blocks):
    n_f, heights, radii, cells = fields.shape
    w = HALO
    band = lax.axis_index("rad")
    first_row = band * radii
    total_rows = rotation.shape[0]
    packed = jnp.concatenate([fields.reshape(n_f * heights, radii, cells), viscosity[None]], axis=0)
    ext = exchange_halo(packed, w)
    u0 = ext[: n_f * heights].reshape(n_f, heights, radii + 2 * w, cells + 2 * w)
    visc = ext[n_f * heights]
    rot = jnp.concatenate([jnp.zeros((w,), rotation.dtype), rotation, jnp.zeros((w,), rotation.dtype)])
    spin = lax.dynamic_slice_in_dim(rot, first_row, radii + 2 * w)[:, None]
    row = first_row - w + lax.iota(jnp.int32, radii + 2 * w)
    inside = ((row >= 0) & (row < total_rows))[:, None]

    def trim(x, k):
        return x[..., k : x.shape[-2] - k, k : x.shape[-1] - k]

    def rates_at(state, k):
        return rates(state, trim(visc, k), spin[k : spin.shape[0] - k])

    def keep(state, k):
        return jnp.where(inside[k : inside.shape[0] - k], state, 0.0)

    state = u0
    first = keep(trim(state, 1) + time_step * rates_at(state, 1), 1)
    second = keep(0.75 * trim(state, 2) + 0.25 * (trim(first, 1) + time_step * rates_at(first, 2)), 2)
    state = trim(state, 3) / 3.0 + 2.0 / 3.0 * (trim(second, 1) + time_step * rates_at(second, 3))
    for t in range(shift_blocks.shape[0]):
        state = advect(state, shift_blocks[t], first_row, w)
    return state


def solution(mesh):
    return jax.shard_map(
        body,
        mesh=mesh,
        in_specs=(P(None, None, "rad", "azi"), P("rad", "azi"), P(), P()),
        out_specs=P(None, None, "rad", "azi"),
        check_vma=False,
    )
```

```python
import jax
import jax.numpy as jnp
from jax import lax
from jax.sharding import PartitionSpec as P

BLOCK = 64
HALO = 3


time_step = 0.3


def exchange_halo(cells, tail, width):
    n_r = lax.axis_size("rad")
    n_a = lax.axis_size("azi")
    up = [(i, i + 1) for i in range(n_r - 1)]
    down = [(i + 1, i) for i in range(n_r - 1)]
    fwd = [(i, (i + 1) % n_a) for i in range(n_a)]
    behind = lax.ppermute(tail, "azi", fwd)
    wide = jnp.concatenate([behind, cells], axis=2)
    south = lax.ppermute(wide[:, -width:, :], "rad", up)
    north = lax.ppermute(wide[:, :width, :], "rad", down)
    return jnp.concatenate([south, wide, north], axis=1)


def rates(state, viscosity, spin):
    centre = state[:, :, 1:-1, 1:-1]
    north = state[:, :, 2:, 1:-1]
    south = state[:, :, :-2, 1:-1]
    ahead = state[:, :, 1:-1, 2:]
    behind = state[:, :, 1:-1, :-2]
    above = jnp.concatenate([centre[:, 1:], centre[:, -1:]], axis=1)
    below = jnp.concatenate([centre[:, :1], centre[:, :-1]], axis=1)
    spread = viscosity * (north + south + ahead + behind + above + below - 6.0 * centre)
    radial_grad = 0.5 * (north - south)
    azimuth_grad = 0.5 * (ahead - behind)
    rate_density = spread[0] - radial_grad[1] - azimuth_grad[2]
    rate_radial = spread[1] - radial_grad[0] + 2.0 * spin * centre[2]
    rate_azimuth = spread[2] - azimuth_grad[0] - 0.5 * spin * centre[1]
    return jnp.stack([rate_density, rate_radial, rate_azimuth])


def advect(state, shift_row, first_row, lag):
    fields, heights, radii, cells = state.shape
    lines = jnp.swapaxes(state.reshape(fields, heights * radii, cells), 0, 1)
    ring = lax.all_to_all(lines, "azi", 0, 0, tiled=True)
    ring = jnp.concatenate([ring[:, :, lag:], jnp.roll(ring, -1, axis=0)[:, :, :lag]], axis=2)
    chunks = ring.shape[0]
    me = lax.axis_index("azi")
    shift = lax.dynamic_index_in_dim(shift_row, first_row + me % radii, keepdims=False)
    per_chunk = cells // BLOCK
    count = chunks * per_chunk
    shift = shift % count
    whole = shift // per_chunk
    part = shift % per_chunk
    doubled = jnp.concatenate([ring, ring], axis=0)
    lane = lax.broadcasted_iota(jnp.int32, ring.shape, 2)
    base = lax.dynamic_slice_in_dim(doubled, (chunks - whole) % chunks, chunks, 0)
    earlier = lax.dynamic_slice_in_dim(doubled, (chunks - whole - 1) % chunks, chunks, 0)
    rolled = base
    for step in range(1, per_chunk):
        mixed = jnp.roll(jnp.where(lane < cells - step * BLOCK, base, earlier), step * BLOCK, axis=2)
        rolled = jnp.where(part == step, mixed, rolled)
    back = lax.all_to_all(rolled, "azi", 0, 0, tiled=True)
    return jnp.swapaxes(back, 0, 1).reshape(fields, heights, radii, cells)


def body(fields, viscosity, rotation, shift_blocks):
    n_f, heights, radii, cells = fields.shape
    w = HALO
    band = lax.axis_index("rad")
    first_row = band * radii
    total_rows = rotation.shape[0]
    packed = jnp.concatenate([fields.reshape(n_f * heights, radii, cells), viscosity[None]], axis=0)
    tail = jnp.concatenate(
        [fields[..., cells - 2 * w :].reshape(n_f * heights, radii, 2 * w), viscosity[None, :, cells - 2 * w :]], axis=0
    )
    ext = exchange_halo(packed, tail, w)
    u0 = ext[: n_f * heights].reshape(n_f, heights, radii + 2 * w, cells + 2 * w)
    visc = ext[n_f * heights]
    rot = jnp.concatenate([jnp.zeros((w,), rotation.dtype), rotation, jnp.zeros((w,), rotation.dtype)])
    spin = lax.dynamic_slice_in_dim(rot, first_row, radii + 2 * w)[:, None]
    row = first_row - w + lax.iota(jnp.int32, radii + 2 * w)
    inside = ((row >= 0) & (row < total_rows))[:, None]

    def trim(x, k):
        return x[..., k : x.shape[-2] - k, k : x.shape[-1] - k]

    def rates_at(state, k):
        return rates(state, trim(visc, k), spin[k : spin.shape[0] - k])

    def keep(state, k):
        return jnp.where(inside[k : inside.shape[0] - k], state, 0.0)

    state = u0
    first = keep(trim(state, 1) + time_step * rates_at(state, 1), 1)
    second = keep(0.75 * trim(state, 2) + 0.25 * (trim(first, 1) + time_step * rates_at(first, 2)), 2)
    state = trim(state, 3) / 3.0 + 2.0 / 3.0 * (trim(second, 1) + time_step * rates_at(second, 3))
    for t in range(shift_blocks.shape[0]):
        state = advect(state, shift_blocks[t], first_row, w)
    return state


def solution(mesh):
    return jax.shard_map(
        body,
        mesh=mesh,
        in_specs=(P(None, None, "rad", "azi"), P("rad", "azi"), P(), P()),
        out_specs=P(None, None, "rad", "azi"),
        check_vma=False,
    )
```

```python
import jax
import jax.numpy as jnp
from jax import lax
from jax.sharding import PartitionSpec as P

BLOCK = 64
HALO = 3


time_step = 0.3


def exchange_halo(cells, tail, width):
    n_r = lax.axis_size("rad")
    n_a = lax.axis_size("azi")
    up = [(i, i + 1) for i in range(n_r - 1)]
    down = [(i + 1, i) for i in range(n_r - 1)]
    behind = tail
    wide = jnp.concatenate([behind, cells], axis=2)
    south = lax.ppermute(wide[:, -width:, :], "rad", up)
    north = lax.ppermute(wide[:, :width, :], "rad", down)
    return jnp.concatenate([south, wide, north], axis=1)


def rates(state, viscosity, spin):
    centre = state[:, :, 1:-1, 1:-1]
    north = state[:, :, 2:, 1:-1]
    south = state[:, :, :-2, 1:-1]
    ahead = state[:, :, 1:-1, 2:]
    behind = state[:, :, 1:-1, :-2]
    above = jnp.concatenate([centre[:, 1:], centre[:, -1:]], axis=1)
    below = jnp.concatenate([centre[:, :1], centre[:, :-1]], axis=1)
    spread = viscosity * (north + south + ahead + behind + above + below - 6.0 * centre)
    radial_grad = 0.5 * (north - south)
    azimuth_grad = 0.5 * (ahead - behind)
    rate_density = spread[0] - radial_grad[1] - azimuth_grad[2]
    rate_radial = spread[1] - radial_grad[0] + 2.0 * spin * centre[2]
    rate_azimuth = spread[2] - azimuth_grad[0] - 0.5 * spin * centre[1]
    return jnp.stack([rate_density, rate_radial, rate_azimuth])


def advect(state, shift_row, first_row, lag):
    fields, heights, radii, cells = state.shape
    lines = jnp.swapaxes(state.reshape(fields, heights * radii, cells), 0, 1)
    ring = lax.all_to_all(lines, "azi", 0, 0, tiled=True)
    ring = jnp.concatenate([ring[:, :, lag:], jnp.roll(ring, -1, axis=0)[:, :, :lag]], axis=2)
    chunks = ring.shape[0]
    me = lax.axis_index("azi")
    shift = lax.dynamic_index_in_dim(shift_row, first_row + me % radii, keepdims=False)
    per_chunk = cells // BLOCK
    count = chunks * per_chunk
    shift = shift % count
    whole = shift // per_chunk
    part = shift % per_chunk
    doubled = jnp.concatenate([ring, ring], axis=0)
    lane = lax.broadcasted_iota(jnp.int32, ring.shape, 2)
    base = lax.dynamic_slice_in_dim(doubled, (chunks - whole) % chunks, chunks, 0)
    earlier = lax.dynamic_slice_in_dim(doubled, (chunks - whole - 1) % chunks, chunks, 0)
    rolled = base
    for step in range(1, per_chunk):
        mixed = jnp.roll(jnp.where(lane < cells - step * BLOCK, base, earlier), step * BLOCK, axis=2)
        rolled = jnp.where(part == step, mixed, rolled)
    back = lax.all_to_all(rolled, "azi", 0, 0, tiled=True)
    return jnp.swapaxes(back, 0, 1).reshape(fields, heights, radii, cells)


def body(fields, viscosity, rotation, shift_blocks):
    n_f, heights, radii, cells = fields.shape
    w = HALO
    band = lax.axis_index("rad")
    first_row = band * radii
    total_rows = rotation.shape[0]
    packed = jnp.concatenate([fields.reshape(n_f * heights, radii, cells), viscosity[None]], axis=0)
    n_a = lax.axis_size("azi")
    got_f, got_v = lax.ppermute((fields, viscosity), "azi", [(i, (i + 1) % n_a) for i in range(n_a)])
    tail = jnp.concatenate(
        [got_f[..., cells - 2 * w :].reshape(n_f * heights, radii, 2 * w), got_v[None, :, cells - 2 * w :]], axis=0
    )
    ext = exchange_halo(packed, tail, w)
    u0 = ext[: n_f * heights].reshape(n_f, heights, radii + 2 * w, cells + 2 * w)
    visc = ext[n_f * heights]
    rot = jnp.concatenate([jnp.zeros((w,), rotation.dtype), rotation, jnp.zeros((w,), rotation.dtype)])
    spin = lax.dynamic_slice_in_dim(rot, first_row, radii + 2 * w)[:, None]
    row = first_row - w + lax.iota(jnp.int32, radii + 2 * w)
    inside = ((row >= 0) & (row < total_rows))[:, None]

    def trim(x, k):
        return x[..., k : x.shape[-2] - k, k : x.shape[-1] - k]

    def rates_at(state, k):
        return rates(state, trim(visc, k), spin[k : spin.shape[0] - k])

    def keep(state, k):
        return jnp.where(inside[k : inside.shape[0] - k], state, 0.0)

    state = u0
    first = keep(trim(state, 1) + time_step * rates_at(state, 1), 1)
    second = keep(0.75 * trim(state, 2) + 0.25 * (trim(first, 1) + time_step * rates_at(first, 2)), 2)
    state = trim(state, 3) / 3.0 + 2.0 / 3.0 * (trim(second, 1) + time_step * rates_at(second, 3))
    for t in range(shift_blocks.shape[0]):
        state = advect(state, shift_blocks[t], first_row, w)
    return state


def solution(mesh):
    return jax.shard_map(
        body,
        mesh=mesh,
        in_specs=(P(None, None, "rad", "azi"), P("rad", "azi"), P(), P()),
        out_specs=P(None, None, "rad", "azi"),
        check_vma=False,
    )
```

```python
import jax
import jax.numpy as jnp
from jax import lax
from jax.sharding import PartitionSpec as P
from jax.experimental import pallas as pl
from jax.experimental.pallas import tpu as pltpu

BLOCK = 64
HALO = 3


time_step = 0.3


def exchange_halo(cells, tail, width):
    n_r = lax.axis_size("rad")
    n_a = lax.axis_size("azi")
    up = [(i, i + 1) for i in range(n_r - 1)]
    down = [(i + 1, i) for i in range(n_r - 1)]
    fwd = [(i, (i + 1) % n_a) for i in range(n_a)]
    behind = lax.ppermute(tail, "azi", fwd)
    wide = jnp.concatenate([behind, cells], axis=2)
    south = lax.ppermute(wide[:, -width:, :], "rad", up)
    north = lax.ppermute(wide[:, :width, :], "rad", down)
    return jnp.concatenate([south, wide, north], axis=1)


def rates(state, viscosity, spin):
    centre = state[:, :, 1:-1, 1:-1]
    north = state[:, :, 2:, 1:-1]
    south = state[:, :, :-2, 1:-1]
    ahead = state[:, :, 1:-1, 2:]
    behind = state[:, :, 1:-1, :-2]
    above = jnp.concatenate([centre[:, 1:], centre[:, -1:]], axis=1)
    below = jnp.concatenate([centre[:, :1], centre[:, :-1]], axis=1)
    spread = viscosity * (north + south + ahead + behind + above + below - 6.0 * centre)
    radial_grad = 0.5 * (north - south)
    azimuth_grad = 0.5 * (ahead - behind)
    rate_density = spread[0] - radial_grad[1] - azimuth_grad[2]
    rate_radial = spread[1] - radial_grad[0] + 2.0 * spin * centre[2]
    rate_azimuth = spread[2] - azimuth_grad[0] - 0.5 * spin * centre[1]
    return jnp.stack([rate_density, rate_radial, rate_azimuth])


def runge_kutta_kernel(ext_ref, spin_ref, inside_ref, out_ref):
    n_f, heights, radii, cells = out_ref.shape
    ext = ext_ref[...]
    planes = n_f * heights
    u0 = ext[:planes]
    visc = ext[planes]
    spin = spin_ref[...]
    inside = inside_ref[...] > 0.0
    rows = ext.shape[1]
    cols = ext.shape[2]

    def rates_all(u):
        north = pltpu.roll(u, rows - 1, 1)
        south = pltpu.roll(u, 1, 1)
        ahead = pltpu.roll(u, cols - 1, 2)
        behind = pltpu.roll(u, 1, 2)
        c = u.reshape(n_f, heights, rows, cols)
        above = jnp.concatenate([c[:, 1:], c[:, heights - 1 :]], axis=1).reshape(u.shape)
        below = jnp.concatenate([c[:, :1], c[:, : heights - 1]], axis=1).reshape(u.shape)
        spread = (visc * (north + south + ahead + behind + above + below - 6.0 * u)).reshape(c.shape)
        radial_grad = (0.5 * (north - south)).reshape(c.shape)
        azimuth_grad = (0.5 * (ahead - behind)).reshape(c.shape)
        rate_density = spread[0] - radial_grad[1] - azimuth_grad[2]
        rate_radial = spread[1] - radial_grad[0] + 2.0 * spin * c[2]
        rate_azimuth = spread[2] - azimuth_grad[0] - 0.5 * spin * c[1]
        return jnp.concatenate([rate_density, rate_radial, rate_azimuth], axis=0)

    first = jnp.where(inside, u0 + time_step * rates_all(u0), 0.0)
    second = jnp.where(inside, 0.75 * u0 + 0.25 * (first + time_step * rates_all(first)), 0.0)
    final = u0 / 3.0 + 2.0 / 3.0 * (second + time_step * rates_all(second))
    final = pltpu.roll(pltpu.roll(final, rows - HALO, 1), cols - HALO, 2)
    out_ref[...] = final[:, :radii, :cells].reshape(out_ref.shape)


def advect(state, shift_row, first_row, lag):
    fields, heights, radii, cells = state.shape
    lines = jnp.swapaxes(state.reshape(fields, heights * radii, cells), 0, 1)
    ring = lax.all_to_all(lines, "azi", 0, 0, tiled=True)
    ring = jnp.concatenate([ring[:, :, lag:], jnp.roll(ring, -1, axis=0)[:, :, :lag]], axis=2)
    chunks = ring.shape[0]
    me = lax.axis_index("azi")
    shift = lax.dynamic_index_in_dim(shift_row, first_row + me % radii, keepdims=False)
    per_chunk = cells // BLOCK
    count = chunks * per_chunk
    shift = shift % count
    whole = shift // per_chunk
    part = shift % per_chunk
    doubled = jnp.concatenate([ring, ring], axis=0)
    lane = lax.broadcasted_iota(jnp.int32, ring.shape, 2)
    base = lax.dynamic_slice_in_dim(doubled, (chunks - whole) % chunks, chunks, 0)
    earlier = lax.dynamic_slice_in_dim(doubled, (chunks - whole - 1) % chunks, chunks, 0)
    rolled = base
    for step in range(1, per_chunk):
        mixed = jnp.roll(jnp.where(lane < cells - step * BLOCK, base, earlier), step * BLOCK, axis=2)
        rolled = jnp.where(part == step, mixed, rolled)
    back = lax.all_to_all(rolled, "azi", 0, 0, tiled=True)
    return jnp.swapaxes(back, 0, 1).reshape(fields, heights, radii, cells)


def body(fields, viscosity, rotation, shift_blocks):
    n_f, heights, radii, cells = fields.shape
    w = HALO
    band = lax.axis_index("rad")
    first_row = band * radii
    total_rows = rotation.shape[0]
    packed = jnp.concatenate([fields.reshape(n_f * heights, radii, cells), viscosity[None]], axis=0)
    tail = jnp.concatenate(
        [fields[..., cells - 2 * w :].reshape(n_f * heights, radii, 2 * w), viscosity[None, :, cells - 2 * w :]], axis=0
    )
    ext = exchange_halo(packed, tail, w)
    rot = jnp.concatenate([jnp.zeros((w,), rotation.dtype), rotation, jnp.zeros((w,), rotation.dtype)])
    spin = lax.dynamic_slice_in_dim(rot, first_row, radii + 2 * w)
    row = first_row - w + lax.iota(jnp.int32, radii + 2 * w)
    inside = ((row >= 0) & (row < total_rows)).astype(jnp.float32)
    pad_rows = -(-(radii + 2 * w) // 8) * 8
    pad_cols = -(-(cells + 2 * w) // 128) * 128
    extra = pad_rows - (radii + 2 * w)
    ext = jnp.pad(ext, ((0, 0), (0, extra), (0, pad_cols - cells - 2 * w)))
    spin = jnp.broadcast_to(jnp.pad(spin, (0, extra))[:, None], (pad_rows, pad_cols))
    inside = jnp.broadcast_to(jnp.pad(inside, (0, extra))[:, None], (pad_rows, pad_cols))
    state = pl.pallas_call(
        runge_kutta_kernel,
        out_shape=jax.ShapeDtypeStruct((n_f, heights, radii, cells), fields.dtype),
    )(ext, spin, inside)
    for t in range(shift_blocks.shape[0]):
        state = advect(state, shift_blocks[t], first_row, w)
    return state


def solution(mesh):
    return jax.shard_map(
        body,
        mesh=mesh,
        in_specs=(P(None, None, "rad", "azi"), P("rad", "azi"), P(), P()),
        out_specs=P(None, None, "rad", "azi"),
        check_vma=False,
    )
```

```python
import jax
import jax.numpy as jnp
from jax import lax
from jax.sharding import Mesh, PartitionSpec as P

BLOCK = 64
HALO = 3
AZI = ("zh", "xy")


time_step = 0.3


def exchange_halo(cells, tail, width):
    n_r = lax.axis_size("rad")
    n_a = lax.axis_size(AZI)
    up = [(i, i + 1) for i in range(n_r - 1)]
    down = [(i + 1, i) for i in range(n_r - 1)]
    fwd = [(i, (i + 1) % n_a) for i in range(n_a)]
    behind = lax.ppermute(tail, AZI, fwd)
    wide = jnp.concatenate([behind, cells], axis=2)
    south = lax.ppermute(wide[:, -width:, :], "rad", up)
    north = lax.ppermute(wide[:, :width, :], "rad", down)
    return jnp.concatenate([south, wide, north], axis=1)


def rates(state, viscosity, spin):
    centre = state[:, :, 1:-1, 1:-1]
    north = state[:, :, 2:, 1:-1]
    south = state[:, :, :-2, 1:-1]
    ahead = state[:, :, 1:-1, 2:]
    behind = state[:, :, 1:-1, :-2]
    above = jnp.concatenate([centre[:, 1:], centre[:, -1:]], axis=1)
    below = jnp.concatenate([centre[:, :1], centre[:, :-1]], axis=1)
    spread = viscosity * (north + south + ahead + behind + above + below - 6.0 * centre)
    radial_grad = 0.5 * (north - south)
    azimuth_grad = 0.5 * (ahead - behind)
    rate_density = spread[0] - radial_grad[1] - azimuth_grad[2]
    rate_radial = spread[1] - radial_grad[0] + 2.0 * spin * centre[2]
    rate_azimuth = spread[2] - azimuth_grad[0] - 0.5 * spin * centre[1]
    return jnp.stack([rate_density, rate_radial, rate_azimuth])


def advect(state, shift_row, first_row, lag):
    fields, heights, radii, cells = state.shape
    n_lines = heights * radii
    n_half = lax.axis_size("xy")
    per = n_lines // n_half
    lines = jnp.swapaxes(state.reshape(fields, n_lines, cells), 0, 1).reshape(n_half, per * fields, cells)
    ring = lax.all_to_all(lines, "xy", 0, 0, tiled=True)
    other = lax.ppermute(ring, "zh", [(0, 1), (1, 0)])
    upper = lax.axis_index("zh")
    ring = jnp.where(upper == 0, jnp.concatenate([ring, other], axis=0), jnp.concatenate([other, ring], axis=0))
    chunks = ring.shape[0]
    ring = ring.reshape(chunks, per, fields, cells)
    ring = jnp.concatenate([ring[..., lag:], jnp.roll(ring, -1, axis=0)[..., :lag]], axis=-1)
    me = lax.axis_index("xy")
    per_chunk = cells // BLOCK
    count = chunks * per_chunk
    doubled = jnp.concatenate([ring, ring], axis=0)
    lane = lax.broadcasted_iota(jnp.int32, (chunks, fields, cells), 2)
    mine = []
    for t in range(per):
        line = doubled[:, t]
        shift = lax.dynamic_index_in_dim(shift_row, first_row + (me * per + t) % radii, keepdims=False)
        shift = shift % count
        whole = shift // per_chunk
        part = shift % per_chunk
        base = lax.dynamic_slice_in_dim(line, (chunks - whole) % chunks, chunks, 0)
        earlier = lax.dynamic_slice_in_dim(line, (chunks - whole - 1) % chunks, chunks, 0)
        rolled = base
        for step in range(1, per_chunk):
            mixed = jnp.roll(jnp.where(lane < cells - step * BLOCK, base, earlier), step * BLOCK, axis=2)
            rolled = jnp.where(part == step, mixed, rolled)
        mine.append(lax.dynamic_slice_in_dim(rolled, upper * n_half, n_half, 0))
    out = jnp.stack(mine, axis=1).reshape(n_half, per * fields, cells)
    back = lax.all_to_all(out, "xy", 0, 0, tiled=True).reshape(n_lines, fields, cells)
    return jnp.swapaxes(back, 0, 1).reshape(fields, heights, radii, cells)


def body(fields, viscosity, rotation, shift_blocks):
    n_f, heights, radii, cells = fields.shape
    w = HALO
    band = lax.axis_index("rad")
    first_row = band * radii
    total_rows = rotation.shape[0]
    packed = jnp.concatenate([fields.reshape(n_f * heights, radii, cells), viscosity[None]], axis=0)
    tail = jnp.concatenate(
        [fields[..., cells - 2 * w :].reshape(n_f * heights, radii, 2 * w), viscosity[None, :, cells - 2 * w :]], axis=0
    )
    ext = exchange_halo(packed, tail, w)
    u0 = ext[: n_f * heights].reshape(n_f, heights, radii + 2 * w, cells + 2 * w)
    visc = ext[n_f * heights]
    rot = jnp.concatenate([jnp.zeros((w,), rotation.dtype), rotation, jnp.zeros((w,), rotation.dtype)])
    spin = lax.dynamic_slice_in_dim(rot, first_row, radii + 2 * w)[:, None]
    row = first_row - w + lax.iota(jnp.int32, radii + 2 * w)
    inside = ((row >= 0) & (row < total_rows))[:, None]

    def trim(x, k):
        return x[..., k : x.shape[-2] - k, k : x.shape[-1] - k]

    def rates_at(state, k):
        return rates(state, trim(visc, k), spin[k : spin.shape[0] - k])

    def keep(state, k):
        return jnp.where(inside[k : inside.shape[0] - k], state, 0.0)

    state = u0
    first = keep(trim(state, 1) + time_step * rates_at(state, 1), 1)
    second = keep(0.75 * trim(state, 2) + 0.25 * (trim(first, 1) + time_step * rates_at(first, 2)), 2)
    state = trim(state, 3) / 3.0 + 2.0 / 3.0 * (trim(second, 1) + time_step * rates_at(second, 3))
    for t in range(shift_blocks.shape[0]):
        state = advect(state, shift_blocks[t], first_row, w)
    return state


def solution(mesh):
    n_r, n_a = mesh.devices.shape
    halves = Mesh(mesh.devices.reshape(n_r, 2, n_a // 2), ("rad",) + AZI)
    return jax.shard_map(
        body,
        mesh=halves,
        in_specs=(P(None, None, "rad", AZI), P("rad", AZI), P(), P()),
        out_specs=P(None, None, "rad", AZI),
        check_vma=False,
    )
```

```python
import jax
import jax.numpy as jnp
from jax import lax
from jax.sharding import Mesh, PartitionSpec as P

BLOCK = 64
HALO = 3
AZI = ("zh", "xy")


time_step = 0.3


def exchange_halo(cells, tail, width):
    n_r = lax.axis_size("rad")
    n_a = lax.axis_size(AZI)
    up = [(i, i + 1) for i in range(n_r - 1)]
    down = [(i + 1, i) for i in range(n_r - 1)]
    fwd = [(i, (i + 1) % n_a) for i in range(n_a)]
    behind = lax.ppermute(tail, AZI, fwd)
    wide = jnp.concatenate([behind, cells], axis=2)
    south = lax.ppermute(wide[:, -width:, :], "rad", up)
    north = lax.ppermute(wide[:, :width, :], "rad", down)
    return jnp.concatenate([south, wide, north], axis=1)


def rates(state, viscosity, spin):
    centre = state[:, :, 1:-1, 1:-1]
    north = state[:, :, 2:, 1:-1]
    south = state[:, :, :-2, 1:-1]
    ahead = state[:, :, 1:-1, 2:]
    behind = state[:, :, 1:-1, :-2]
    above = jnp.concatenate([centre[:, 1:], centre[:, -1:]], axis=1)
    below = jnp.concatenate([centre[:, :1], centre[:, :-1]], axis=1)
    spread = viscosity * (north + south + ahead + behind + above + below - 6.0 * centre)
    radial_grad = 0.5 * (north - south)
    azimuth_grad = 0.5 * (ahead - behind)
    rate_density = spread[0] - radial_grad[1] - azimuth_grad[2]
    rate_radial = spread[1] - radial_grad[0] + 2.0 * spin * centre[2]
    rate_azimuth = spread[2] - azimuth_grad[0] - 0.5 * spin * centre[1]
    return jnp.stack([rate_density, rate_radial, rate_azimuth])


def advect(state, shift_row, first_row, lag):
    fields, heights, radii, cells = state.shape
    n_lines = heights * radii
    n_half = lax.axis_size("xy")
    per = n_lines // n_half
    lines = jnp.swapaxes(state.reshape(fields, n_lines, cells), 0, 1).reshape(per, n_half, fields, cells)
    lines = jnp.swapaxes(lines, 0, 1).reshape(n_half, per * fields, cells)
    ring = lax.all_to_all(lines, "xy", 0, 0, tiled=True)
    other = lax.ppermute(ring, "zh", [(0, 1), (1, 0)])
    upper = lax.axis_index("zh")
    ring = jnp.where(upper == 0, jnp.concatenate([ring, other], axis=0), jnp.concatenate([other, ring], axis=0))
    chunks = ring.shape[0]
    ring = ring.reshape(chunks, per, fields, cells)
    ring = jnp.concatenate([ring[..., lag:], jnp.roll(ring, -1, axis=0)[..., :lag]], axis=-1)
    me = lax.axis_index("xy")
    per_chunk = cells // BLOCK
    count = chunks * per_chunk
    doubled = jnp.concatenate([ring, ring], axis=0)
    lane = lax.broadcasted_iota(jnp.int32, (chunks, fields, cells), 2)
    mine = []
    for t in range(per):
        line = doubled[:, t]
        shift = lax.dynamic_index_in_dim(shift_row, first_row + (t * n_half + me) % radii, keepdims=False)
        shift = shift % count
        whole = shift // per_chunk
        part = shift % per_chunk
        base = lax.dynamic_slice_in_dim(line, (chunks - whole) % chunks, chunks, 0)
        earlier = lax.dynamic_slice_in_dim(line, (chunks - whole - 1) % chunks, chunks, 0)
        rolled = base
        for step in range(1, per_chunk):
            mixed = jnp.roll(jnp.where(lane < cells - step * BLOCK, base, earlier), step * BLOCK, axis=2)
            rolled = jnp.where(part == step, mixed, rolled)
        mine.append(lax.dynamic_slice_in_dim(rolled, upper * n_half, n_half, 0))
    out = jnp.stack(mine, axis=1).reshape(n_half, per * fields, cells)
    back = lax.all_to_all(out, "xy", 0, 0, tiled=True).reshape(n_half, per, fields, cells)
    back = jnp.swapaxes(back, 0, 1).reshape(n_lines, fields, cells)
    return jnp.swapaxes(back, 0, 1).reshape(fields, heights, radii, cells)


def body(fields, viscosity, rotation, shift_blocks):
    n_f, heights, radii, cells = fields.shape
    w = HALO
    band = lax.axis_index("rad")
    first_row = band * radii
    total_rows = rotation.shape[0]
    packed = jnp.concatenate([fields.reshape(n_f * heights, radii, cells), viscosity[None]], axis=0)
    tail = jnp.concatenate(
        [fields[..., cells - 2 * w :].reshape(n_f * heights, radii, 2 * w), viscosity[None, :, cells - 2 * w :]], axis=0
    )
    ext = exchange_halo(packed, tail, w)
    u0 = ext[: n_f * heights].reshape(n_f, heights, radii + 2 * w, cells + 2 * w)
    visc = ext[n_f * heights]
    rot = jnp.concatenate([jnp.zeros((w,), rotation.dtype), rotation, jnp.zeros((w,), rotation.dtype)])
    spin = lax.dynamic_slice_in_dim(rot, first_row, radii + 2 * w)[:, None]
    row = first_row - w + lax.iota(jnp.int32, radii + 2 * w)
    inside = ((row >= 0) & (row < total_rows))[:, None]

    def trim(x, k):
        return x[..., k : x.shape[-2] - k, k : x.shape[-1] - k]

    def rates_at(state, k):
        return rates(state, trim(visc, k), spin[k : spin.shape[0] - k])

    def keep(state, k):
        return jnp.where(inside[k : inside.shape[0] - k], state, 0.0)

    state = u0
    first = keep(trim(state, 1) + time_step * rates_at(state, 1), 1)
    second = keep(0.75 * trim(state, 2) + 0.25 * (trim(first, 1) + time_step * rates_at(first, 2)), 2)
    state = trim(state, 3) / 3.0 + 2.0 / 3.0 * (trim(second, 1) + time_step * rates_at(second, 3))
    for t in range(shift_blocks.shape[0]):
        state = advect(state, shift_blocks[t], first_row, w)
    return state


def solution(mesh):
    n_r, n_a = mesh.devices.shape
    halves = Mesh(mesh.devices.reshape(n_r, 2, n_a // 2), ("rad",) + AZI)
    return jax.shard_map(
        body,
        mesh=halves,
        in_specs=(P(None, None, "rad", AZI), P("rad", AZI), P(), P()),
        out_specs=P(None, None, "rad", AZI),
        check_vma=False,
    )
```

```python
import jax
import jax.numpy as jnp
from jax import lax
from jax.sharding import Mesh, PartitionSpec as P

BLOCK = 64
HALO = 3
AZI = ("zh", "xy")


time_step = 0.3


def exchange_halo(cells, tail, width):
    n_r = lax.axis_size("rad")
    n_a = lax.axis_size(AZI)
    up = [(i, i + 1) for i in range(n_r - 1)]
    down = [(i + 1, i) for i in range(n_r - 1)]
    fwd = [(i, (i + 1) % n_a) for i in range(n_a)]
    behind = lax.ppermute(tail, AZI, fwd)
    wide = jnp.concatenate([behind, cells], axis=2)
    south = lax.ppermute(wide[:, -width:, :], "rad", up)
    north = lax.ppermute(wide[:, :width, :], "rad", down)
    return jnp.concatenate([south, wide, north], axis=1)


def rates(state, viscosity, spin):
    centre = state[:, :, 1:-1, 1:-1]
    north = state[:, :, 2:, 1:-1]
    south = state[:, :, :-2, 1:-1]
    ahead = state[:, :, 1:-1, 2:]
    behind = state[:, :, 1:-1, :-2]
    above = jnp.concatenate([centre[:, 1:], centre[:, -1:]], axis=1)
    below = jnp.concatenate([centre[:, :1], centre[:, :-1]], axis=1)
    spread = viscosity * (north + south + ahead + behind + above + below - 6.0 * centre)
    radial_grad = 0.5 * (north - south)
    azimuth_grad = 0.5 * (ahead - behind)
    rate_density = spread[0] - radial_grad[1] - azimuth_grad[2]
    rate_radial = spread[1] - radial_grad[0] + 2.0 * spin * centre[2]
    rate_azimuth = spread[2] - azimuth_grad[0] - 0.5 * spin * centre[1]
    return jnp.stack([rate_density, rate_radial, rate_azimuth])


def advect(state, shift_row, first_row, lag):
    fields, heights, radii, cells = state.shape
    n_lines = heights * radii
    n_half = lax.axis_size("xy")
    per = n_lines // n_half
    lines = jnp.swapaxes(state.reshape(fields, n_lines, cells), 0, 1).reshape(per, n_half, fields, cells)
    lines = jnp.swapaxes(lines, 0, 1).reshape(n_half, per * fields, cells)
    ring = lax.all_to_all(lines, "xy", 0, 0, tiled=True)
    other = lax.ppermute(ring, "zh", [(0, 1), (1, 0)])
    upper = lax.axis_index("zh")
    ring = jnp.where(upper == 0, jnp.concatenate([ring, other], axis=0), jnp.concatenate([other, ring], axis=0))
    chunks = ring.shape[0]
    ring = ring.reshape(chunks, per, fields, cells)
    ring = jnp.concatenate([ring[..., lag:], jnp.roll(ring, -1, axis=0)[..., :lag]], axis=-1)
    me = lax.axis_index("xy")
    per_chunk = cells // BLOCK
    count = chunks * per_chunk
    doubled = jnp.concatenate([ring, ring], axis=0)
    lane = lax.broadcasted_iota(jnp.int32, (chunks, fields, cells), 2)
    mine = []
    for t in range(per):
        line = doubled[:, t]
        shift = lax.dynamic_index_in_dim(shift_row, first_row + (t * n_half + me) % radii, keepdims=False)
        shift = shift % count
        whole = shift // per_chunk
        part = shift % per_chunk
        base = lax.dynamic_slice_in_dim(line, (chunks - whole) % chunks, chunks, 0)
        earlier = lax.dynamic_slice_in_dim(line, (chunks - whole - 1) % chunks, chunks, 0)
        rolled = base
        for step in range(1, per_chunk):
            mixed = jnp.roll(jnp.where(lane < cells - step * BLOCK, base, earlier), step * BLOCK, axis=2)
            rolled = jnp.where(part == step, mixed, rolled)
        mine.append(lax.dynamic_slice_in_dim(rolled, upper * n_half, n_half, 0))
    out = jnp.stack(mine, axis=1).reshape(n_half, per * fields, cells)
    back = lax.all_to_all(out, "xy", 0, 0, tiled=True).reshape(n_half, per, fields, cells)
    back = jnp.swapaxes(back, 0, 1).reshape(n_lines, fields, cells)
    return jnp.swapaxes(back, 0, 1).reshape(fields, heights, radii, cells)


def body(fields, viscosity, rotation, shift_blocks):
    n_f, heights, radii, cells = fields.shape
    w = HALO
    band = lax.axis_index("rad")
    first_row = band * radii
    total_rows = rotation.shape[0]
    packed = jnp.concatenate([fields.reshape(n_f * heights, radii, cells), viscosity[None]], axis=0)
    tail = jnp.concatenate([fields.reshape(n_f * heights, radii, cells), viscosity[None]], axis=0)[..., cells - 2 * w :]
    ext = exchange_halo(packed, tail, w)
    u0 = ext[: n_f * heights].reshape(n_f, heights, radii + 2 * w, cells + 2 * w)
    visc = ext[n_f * heights]
    rot = jnp.concatenate([jnp.zeros((w,), rotation.dtype), rotation, jnp.zeros((w,), rotation.dtype)])
    spin = lax.dynamic_slice_in_dim(rot, first_row, radii + 2 * w)[:, None]
    row = first_row - w + lax.iota(jnp.int32, radii + 2 * w)
    inside = ((row >= 0) & (row < total_rows))[:, None]

    def trim(x, k):
        return x[..., k : x.shape[-2] - k, k : x.shape[-1] - k]

    def rates_at(state, k):
        return rates(state, trim(visc, k), spin[k : spin.shape[0] - k])

    def keep(state, k):
        return jnp.where(inside[k : inside.shape[0] - k], state, 0.0)

    state = u0
    first = keep(trim(state, 1) + time_step * rates_at(state, 1), 1)
    second = keep(0.75 * trim(state, 2) + 0.25 * (trim(first, 1) + time_step * rates_at(first, 2)), 2)
    state = trim(state, 3) / 3.0 + 2.0 / 3.0 * (trim(second, 1) + time_step * rates_at(second, 3))
    for t in range(shift_blocks.shape[0]):
        state = advect(state, shift_blocks[t], first_row, w)
    return state


def solution(mesh):
    n_r, n_a = mesh.devices.shape
    halves = Mesh(mesh.devices.reshape(n_r, 2, n_a // 2), ("rad",) + AZI)
    return jax.shard_map(
        body,
        mesh=halves,
        in_specs=(P(None, None, "rad", AZI), P("rad", AZI), P(), P()),
        out_specs=P(None, None, "rad", AZI),
        check_vma=False,
    )
```

```python
import jax
import jax.numpy as jnp
from jax import lax
from jax.sharding import Mesh, PartitionSpec as P

BLOCK = 64
HALO = 3
OUTER = ("zh", "xh")
INNER = ("xl", "y")
AZI = OUTER + INNER


time_step = 0.3


def exchange_halo(cells, tail, width):
    n_r = lax.axis_size("rad")
    n_a = lax.axis_size(AZI)
    up = [(i, i + 1) for i in range(n_r - 1)]
    down = [(i + 1, i) for i in range(n_r - 1)]
    fwd = [(i, (i + 1) % n_a) for i in range(n_a)]
    behind = lax.ppermute(tail, AZI, fwd)
    wide = jnp.concatenate([behind, cells], axis=2)
    south = lax.ppermute(wide[:, -width:, :], "rad", up)
    north = lax.ppermute(wide[:, :width, :], "rad", down)
    return jnp.concatenate([south, wide, north], axis=1)


def rates(state, viscosity, spin):
    centre = state[:, :, 1:-1, 1:-1]
    north = state[:, :, 2:, 1:-1]
    south = state[:, :, :-2, 1:-1]
    ahead = state[:, :, 1:-1, 2:]
    behind = state[:, :, 1:-1, :-2]
    above = jnp.concatenate([centre[:, 1:], centre[:, -1:]], axis=1)
    below = jnp.concatenate([centre[:, :1], centre[:, :-1]], axis=1)
    spread = viscosity * (north + south + ahead + behind + above + below - 6.0 * centre)
    radial_grad = 0.5 * (north - south)
    azimuth_grad = 0.5 * (ahead - behind)
    rate_density = spread[0] - radial_grad[1] - azimuth_grad[2]
    rate_radial = spread[1] - radial_grad[0] + 2.0 * spin * centre[2]
    rate_azimuth = spread[2] - azimuth_grad[0] - 0.5 * spin * centre[1]
    return jnp.stack([rate_density, rate_radial, rate_azimuth])


def advect(state, shift_row, first_row, lag):
    fields, heights, radii, cells = state.shape
    n_lines = heights * radii
    n_grp = lax.axis_size(INNER)
    per = n_lines // n_grp
    lines = jnp.swapaxes(state.reshape(fields, n_lines, cells), 0, 1).reshape(per, n_grp, fields, cells)
    lines = jnp.swapaxes(lines, 0, 1).reshape(n_grp, per * fields, cells)
    ring = lax.all_to_all(lines, INNER, 0, 0, tiled=True)
    start = 0
    for axis in OUTER[::-1]:
        other = lax.ppermute(ring, axis, [(0, 1), (1, 0)])
        side = lax.axis_index(axis)
        start = start + side * ring.shape[0]
        ring = jnp.where(side == 0, jnp.concatenate([ring, other], axis=0), jnp.concatenate([other, ring], axis=0))
    chunks = ring.shape[0]
    ring = ring.reshape(chunks, per, fields, cells)
    ring = jnp.concatenate([ring[..., lag:], jnp.roll(ring, -1, axis=0)[..., :lag]], axis=-1)
    me = lax.axis_index(INNER)
    per_chunk = cells // BLOCK
    count = chunks * per_chunk
    doubled = jnp.concatenate([ring, ring], axis=0)
    lane = lax.broadcasted_iota(jnp.int32, (chunks, fields, cells), 2)
    mine = []
    for t in range(per):
        line = doubled[:, t]
        shift = lax.dynamic_index_in_dim(shift_row, first_row + (t * n_grp + me) % radii, keepdims=False)
        shift = shift % count
        whole = shift // per_chunk
        part = shift % per_chunk
        base = lax.dynamic_slice_in_dim(line, (chunks - whole) % chunks, chunks, 0)
        earlier = lax.dynamic_slice_in_dim(line, (chunks - whole - 1) % chunks, chunks, 0)
        rolled = base
        for step in range(1, per_chunk):
            mixed = jnp.roll(jnp.where(lane < cells - step * BLOCK, base, earlier), step * BLOCK, axis=2)
            rolled = jnp.where(part == step, mixed, rolled)
        mine.append(lax.dynamic_slice_in_dim(rolled, start, n_grp, 0))
    out = jnp.stack(mine, axis=1).reshape(n_grp, per * fields, cells)
    back = lax.all_to_all(out, INNER, 0, 0, tiled=True).reshape(n_grp, per, fields, cells)
    back = jnp.swapaxes(back, 0, 1).reshape(n_lines, fields, cells)
    return jnp.swapaxes(back, 0, 1).reshape(fields, heights, radii, cells)


def body(fields, viscosity, rotation, shift_blocks):
    n_f, heights, radii, cells = fields.shape
    w = HALO
    band = lax.axis_index("rad")
    first_row = band * radii
    total_rows = rotation.shape[0]
    packed = jnp.concatenate([fields.reshape(n_f * heights, radii, cells), viscosity[None]], axis=0)
    tail = jnp.concatenate(
        [fields[..., cells - 2 * w :].reshape(n_f * heights, radii, 2 * w), viscosity[None, :, cells - 2 * w :]], axis=0
    )
    ext = exchange_halo(packed, tail, w)
    u0 = ext[: n_f * heights].reshape(n_f, heights, radii + 2 * w, cells + 2 * w)
    visc = ext[n_f * heights]
    rot = jnp.concatenate([jnp.zeros((w,), rotation.dtype), rotation, jnp.zeros((w,), rotation.dtype)])
    spin = lax.dynamic_slice_in_dim(rot, first_row, radii + 2 * w)[:, None]
    row = first_row - w + lax.iota(jnp.int32, radii + 2 * w)
    inside = ((row >= 0) & (row < total_rows))[:, None]

    def trim(x, k):
        return x[..., k : x.shape[-2] - k, k : x.shape[-1] - k]

    def rates_at(state, k):
        return rates(state, trim(visc, k), spin[k : spin.shape[0] - k])

    def keep(state, k):
        return jnp.where(inside[k : inside.shape[0] - k], state, 0.0)

    state = u0
    first = keep(trim(state, 1) + time_step * rates_at(state, 1), 1)
    second = keep(0.75 * trim(state, 2) + 0.25 * (trim(first, 1) + time_step * rates_at(first, 2)), 2)
    state = trim(state, 3) / 3.0 + 2.0 / 3.0 * (trim(second, 1) + time_step * rates_at(second, 3))
    for t in range(shift_blocks.shape[0]):
        state = advect(state, shift_blocks[t], first_row, w)
    return state


def solution(mesh):
    n_r, n_a = mesh.devices.shape
    quarters = Mesh(mesh.devices.reshape(n_r, 2, 2, 2, n_a // 8), ("rad",) + AZI)
    return jax.shard_map(
        body,
        mesh=quarters,
        in_specs=(P(None, None, "rad", AZI), P("rad", AZI), P(), P()),
        out_specs=P(None, None, "rad", AZI),
        check_vma=False,
    )
```

```python
import jax
import jax.numpy as jnp
from jax import lax
from jax.sharding import Mesh, PartitionSpec as P

BLOCK = 64
HALO = 3
AZI = ("zh", "xy")


time_step = 0.3


def exchange_halo(cells, tail, width):
    n_r = lax.axis_size("rad")
    n_a = lax.axis_size(AZI)
    up = [(i, i + 1) for i in range(n_r - 1)]
    down = [(i + 1, i) for i in range(n_r - 1)]
    fwd = [(i, (i + 1) % n_a) for i in range(n_a)]
    behind = lax.ppermute(tail, AZI, fwd)
    wide = jnp.concatenate([behind, cells], axis=2)
    south = lax.ppermute(wide[:, -width:, :], "rad", up)
    north = lax.ppermute(wide[:, :width, :], "rad", down)
    return jnp.concatenate([south, wide, north], axis=1)


def rates(state, viscosity, spin):
    centre = state[:, :, 1:-1, 1:-1]
    north = state[:, :, 2:, 1:-1]
    south = state[:, :, :-2, 1:-1]
    ahead = state[:, :, 1:-1, 2:]
    behind = state[:, :, 1:-1, :-2]
    above = jnp.concatenate([centre[:, 1:], centre[:, -1:]], axis=1)
    below = jnp.concatenate([centre[:, :1], centre[:, :-1]], axis=1)
    spread = viscosity * (north + south + ahead + behind + above + below - 6.0 * centre)
    radial_grad = 0.5 * (north - south)
    azimuth_grad = 0.5 * (ahead - behind)
    rate_density = spread[0] - radial_grad[1] - azimuth_grad[2]
    rate_radial = spread[1] - radial_grad[0] + 2.0 * spin * centre[2]
    rate_azimuth = spread[2] - azimuth_grad[0] - 0.5 * spin * centre[1]
    return jnp.stack([rate_density, rate_radial, rate_azimuth])


def advect(state, shift_row, first_row, lag):
    fields, heights, radii, cells = state.shape
    n_lines = heights * radii
    n_half = lax.axis_size("xy")
    per = n_lines // n_half
    lines = jnp.swapaxes(state.reshape(fields, n_lines, cells), 0, 1).reshape(per, n_half, fields, cells)
    lines = jnp.swapaxes(lines, 0, 1).reshape(n_half, per * fields, cells)
    ring = lax.all_to_all(lines, "xy", 0, 0, tiled=True)
    upper = lax.axis_index("zh")
    empty = jnp.zeros_like(ring)
    ring = jnp.where(upper == 0, jnp.concatenate([ring, empty], axis=0), jnp.concatenate([empty, ring], axis=0))
    chunks = ring.shape[0]
    ring = ring.reshape(chunks, per, fields, cells)
    ring = jnp.concatenate([ring[..., lag:], jnp.roll(ring, -1, axis=0)[..., :lag]], axis=-1)
    me = lax.axis_index("xy")
    per_chunk = cells // BLOCK
    count = chunks * per_chunk
    doubled = jnp.concatenate([ring, ring], axis=0)
    lane = lax.broadcasted_iota(jnp.int32, (chunks, fields, cells), 2)
    moved = []
    for t in range(per):
        line = doubled[:, t]
        shift = lax.dynamic_index_in_dim(shift_row, first_row + (t * n_half + me) % radii, keepdims=False)
        shift = shift % count
        whole = shift // per_chunk
        part = shift % per_chunk
        base = lax.dynamic_slice_in_dim(line, (chunks - whole) % chunks, chunks, 0)
        earlier = lax.dynamic_slice_in_dim(line, (chunks - whole - 1) % chunks, chunks, 0)
        rolled = base
        for step in range(1, per_chunk):
            mixed = jnp.roll(jnp.where(lane < cells - step * BLOCK, base, earlier), step * BLOCK, axis=2)
            rolled = jnp.where(part == step, mixed, rolled)
        moved.append(rolled)
    out = jnp.stack(moved, axis=1).reshape(chunks, per * fields, cells)
    back = lax.all_to_all(out, AZI, 0, 0, tiled=True).reshape(2, n_half, per, fields, cells)
    sender = lax.broadcasted_iota(jnp.int32, (n_half, per), 0)
    t_idx = lax.broadcasted_iota(jnp.int32, (n_half, per), 1)
    k = jnp.take(shift_row, first_row + (t_idx * n_half + sender) % radii) % count
    cell = lax.axis_index(AZI) * cells + lax.broadcasted_iota(jnp.int32, (n_half, per, cells), 2)
    source = (cell - BLOCK * k[:, :, None]) % (chunks * cells)
    lower = (source < n_half * cells - lag) | (source >= chunks * cells - lag)
    kept = jnp.where(lower[:, :, None, :], back[0], back[1])
    kept = jnp.swapaxes(kept, 0, 1).reshape(n_lines, fields, cells)
    return jnp.swapaxes(kept, 0, 1).reshape(fields, heights, radii, cells)


def body(fields, viscosity, rotation, shift_blocks):
    n_f, heights, radii, cells = fields.shape
    w = HALO
    band = lax.axis_index("rad")
    first_row = band * radii
    total_rows = rotation.shape[0]
    packed = jnp.concatenate([fields.reshape(n_f * heights, radii, cells), viscosity[None]], axis=0)
    tail = jnp.concatenate(
        [fields[..., cells - 2 * w :].reshape(n_f * heights, radii, 2 * w), viscosity[None, :, cells - 2 * w :]], axis=0
    )
    ext = exchange_halo(packed, tail, w)
    u0 = ext[: n_f * heights].reshape(n_f, heights, radii + 2 * w, cells + 2 * w)
    visc = ext[n_f * heights]
    rot = jnp.concatenate([jnp.zeros((w,), rotation.dtype), rotation, jnp.zeros((w,), rotation.dtype)])
    spin = lax.dynamic_slice_in_dim(rot, first_row, radii + 2 * w)[:, None]
    row = first_row - w + lax.iota(jnp.int32, radii + 2 * w)
    inside = ((row >= 0) & (row < total_rows))[:, None]

    def trim(x, k):
        return x[..., k : x.shape[-2] - k, k : x.shape[-1] - k]

    def rates_at(state, k):
        return rates(state, trim(visc, k), spin[k : spin.shape[0] - k])

    def keep(state, k):
        return jnp.where(inside[k : inside.shape[0] - k], state, 0.0)

    state = u0
    first = keep(trim(state, 1) + time_step * rates_at(state, 1), 1)
    second = keep(0.75 * trim(state, 2) + 0.25 * (trim(first, 1) + time_step * rates_at(first, 2)), 2)
    state = trim(state, 3) / 3.0 + 2.0 / 3.0 * (trim(second, 1) + time_step * rates_at(second, 3))
    for t in range(shift_blocks.shape[0]):
        state = advect(state, shift_blocks[t], first_row, w)
    return state


def solution(mesh):
    n_r, n_a = mesh.devices.shape
    halves = Mesh(mesh.devices.reshape(n_r, 2, n_a // 2), ("rad",) + AZI)
    return jax.shard_map(
        body,
        mesh=halves,
        in_specs=(P(None, None, "rad", AZI), P("rad", AZI), P(), P()),
        out_specs=P(None, None, "rad", AZI),
        check_vma=False,
    )
```

```python
import jax
import jax.numpy as jnp
from jax import lax
from jax.sharding import Mesh, PartitionSpec as P

BLOCK = 64
HALO = 3
AZI = ("zh", "xy")


time_step = 0.3


def exchange_halo(cells, tail, width):
    n_r = lax.axis_size("rad")
    n_a = lax.axis_size(AZI)
    up = [(i, i + 1) for i in range(n_r - 1)]
    down = [(i + 1, i) for i in range(n_r - 1)]
    fwd = [(i, (i + 1) % n_a) for i in range(n_a)]
    behind = lax.ppermute(tail, AZI, fwd)
    wide = jnp.concatenate([behind, cells], axis=2)
    south = lax.ppermute(wide[:, -width:, :], "rad", up)
    north = lax.ppermute(wide[:, :width, :], "rad", down)
    return jnp.concatenate([south, wide, north], axis=1)


def rates(state, viscosity, spin):
    centre = state[:, :, 1:-1, 1:-1]
    north = state[:, :, 2:, 1:-1]
    south = state[:, :, :-2, 1:-1]
    ahead = state[:, :, 1:-1, 2:]
    behind = state[:, :, 1:-1, :-2]
    above = jnp.concatenate([centre[:, 1:], centre[:, -1:]], axis=1)
    below = jnp.concatenate([centre[:, :1], centre[:, :-1]], axis=1)
    spread = viscosity * (north + south + ahead + behind + above + below - 6.0 * centre)
    radial_grad = 0.5 * (north - south)
    azimuth_grad = 0.5 * (ahead - behind)
    rate_density = spread[0] - radial_grad[1] - azimuth_grad[2]
    rate_radial = spread[1] - radial_grad[0] + 2.0 * spin * centre[2]
    rate_azimuth = spread[2] - azimuth_grad[0] - 0.5 * spin * centre[1]
    return jnp.stack([rate_density, rate_radial, rate_azimuth])


def advect(state, shift_row, first_row, lag):
    fields, heights, radii, cells = state.shape
    n_lines = heights * radii
    n_half = lax.axis_size("xy")
    per = n_lines // n_half
    lines = jnp.swapaxes(state.reshape(fields, n_lines, cells), 0, 1).reshape(per, n_half, fields, cells)
    lines = jnp.swapaxes(lines, 0, 1).reshape(n_half, per * fields, cells)
    ring = lax.all_to_all(lines, "xy", 0, 0, tiled=True)
    other = lax.ppermute(ring, "zh", [(0, 1), (1, 0)])
    upper = lax.axis_index("zh")
    ring = jnp.where(upper == 0, jnp.concatenate([ring, other], axis=0), jnp.concatenate([other, ring], axis=0))
    chunks = ring.shape[0]
    ring = ring.reshape(chunks, per, fields, cells)
    ring = jnp.concatenate([ring[..., lag:], jnp.roll(ring, -1, axis=0)[..., :lag]], axis=-1)
    me = lax.axis_index("xy")
    per_chunk = cells // BLOCK
    count = chunks * per_chunk
    doubled = jnp.concatenate([ring, ring], axis=0)
    groups = [list(range(per))] if n_half % radii == 0 else [[t] for t in range(per)]
    mine = []
    for group in groups:
        line = doubled[:, group[0] : group[-1] + 1]
        lane = lax.broadcasted_iota(jnp.int32, (chunks,) + line.shape[1:], line.ndim - 1)
        shift = lax.dynamic_index_in_dim(shift_row, first_row + (group[0] * n_half + me) % radii, keepdims=False)
        shift = shift % count
        whole = shift // per_chunk
        part = shift % per_chunk
        base = lax.dynamic_slice_in_dim(line, (chunks - whole) % chunks, chunks, 0)
        earlier = lax.dynamic_slice_in_dim(line, (chunks - whole - 1) % chunks, chunks, 0)
        rolled = base
        for step in range(1, per_chunk):
            mixed = jnp.roll(jnp.where(lane < cells - step * BLOCK, base, earlier), step * BLOCK, axis=-1)
            rolled = jnp.where(part == step, mixed, rolled)
        mine.append(lax.dynamic_slice_in_dim(rolled, upper * n_half, n_half, 0))
    out = jnp.concatenate(mine, axis=1).reshape(n_half, per * fields, cells)
    back = lax.all_to_all(out, "xy", 0, 0, tiled=True).reshape(n_half, per, fields, cells)
    back = jnp.swapaxes(back, 0, 1).reshape(n_lines, fields, cells)
    return jnp.swapaxes(back, 0, 1).reshape(fields, heights, radii, cells)


def body(fields, viscosity, rotation, shift_blocks):
    n_f, heights, radii, cells = fields.shape
    w = HALO
    band = lax.axis_index("rad")
    first_row = band * radii
    total_rows = rotation.shape[0]
    packed = jnp.concatenate([fields.reshape(n_f * heights, radii, cells), viscosity[None]], axis=0)
    tail = jnp.concatenate(
        [fields[..., cells - 2 * w :].reshape(n_f * heights, radii, 2 * w), viscosity[None, :, cells - 2 * w :]], axis=0
    )
    ext = exchange_halo(packed, tail, w)
    u0 = ext[: n_f * heights].reshape(n_f, heights, radii + 2 * w, cells + 2 * w)
    visc = ext[n_f * heights]
    rot = jnp.concatenate([jnp.zeros((w,), rotation.dtype), rotation, jnp.zeros((w,), rotation.dtype)])
    spin = lax.dynamic_slice_in_dim(rot, first_row, radii + 2 * w)[:, None]
    row = first_row - w + lax.iota(jnp.int32, radii + 2 * w)
    inside = ((row >= 0) & (row < total_rows))[:, None]

    def trim(x, k):
        return x[..., k : x.shape[-2] - k, k : x.shape[-1] - k]

    def rates_at(state, k):
        return rates(state, trim(visc, k), spin[k : spin.shape[0] - k])

    def keep(state, k):
        return jnp.where(inside[k : inside.shape[0] - k], state, 0.0)

    state = u0
    first = keep(trim(state, 1) + time_step * rates_at(state, 1), 1)
    second = keep(0.75 * trim(state, 2) + 0.25 * (trim(first, 1) + time_step * rates_at(first, 2)), 2)
    state = trim(state, 3) / 3.0 + 2.0 / 3.0 * (trim(second, 1) + time_step * rates_at(second, 3))
    for t in range(shift_blocks.shape[0]):
        state = advect(state, shift_blocks[t], first_row, w)
    return state


def solution(mesh):
    n_r, n_a = mesh.devices.shape
    halves = Mesh(mesh.devices.reshape(n_r, 2, n_a // 2), ("rad",) + AZI)
    return jax.shard_map(
        body,
        mesh=halves,
        in_specs=(P(None, None, "rad", AZI), P("rad", AZI), P(), P()),
        out_specs=P(None, None, "rad", AZI),
        check_vma=False,
    )
```

```python
import jax
import jax.numpy as jnp
from jax import lax
from jax.sharding import Mesh, PartitionSpec as P

BLOCK = 64
HALO = 3
AZI = ("zh", "xy")


time_step = 0.3


def exchange_halo(cells, tail, width):
    n_r = lax.axis_size("rad")
    n_a = lax.axis_size(AZI)
    up = [(i, i + 1) for i in range(n_r - 1)]
    down = [(i + 1, i) for i in range(n_r - 1)]
    fwd = [(i, (i + 1) % n_a) for i in range(n_a)]
    behind = lax.ppermute(tail, AZI, fwd)
    wide = jnp.concatenate([behind, cells], axis=2)
    south = lax.ppermute(wide[:, -width:, :], "rad", up)
    north = lax.ppermute(wide[:, :width, :], "rad", down)
    return jnp.concatenate([south, wide, north], axis=1)


def rates(state, viscosity, spin):
    centre = state[:, :, 1:-1, 1:-1]
    north = state[:, :, 2:, 1:-1]
    south = state[:, :, :-2, 1:-1]
    ahead = state[:, :, 1:-1, 2:]
    behind = state[:, :, 1:-1, :-2]
    above = jnp.concatenate([centre[:, 1:], centre[:, -1:]], axis=1)
    below = jnp.concatenate([centre[:, :1], centre[:, :-1]], axis=1)
    spread = viscosity * (north + south + ahead + behind + above + below - 6.0 * centre)
    radial_grad = 0.5 * (north - south)
    azimuth_grad = 0.5 * (ahead - behind)
    rate_density = spread[0] - radial_grad[1] - azimuth_grad[2]
    rate_radial = spread[1] - radial_grad[0] + 2.0 * spin * centre[2]
    rate_azimuth = spread[2] - azimuth_grad[0] - 0.5 * spin * centre[1]
    return jnp.stack([rate_density, rate_radial, rate_azimuth])


def advect(state, shift_row, first_row, lag):
    fields, heights, radii, cells = state.shape
    n_lines = heights * radii
    n_half = lax.axis_size("xy")
    per = n_lines // n_half
    lines = jnp.swapaxes(state.reshape(fields, n_lines, cells), 0, 1).reshape(per, n_half, fields, cells)
    lines = jnp.swapaxes(lines, 0, 1).reshape(n_half, per * fields, cells)
    ring = lax.all_to_all(lines, "xy", 0, 0, tiled=True)
    other = lax.ppermute(ring, "zh", [(0, 1), (1, 0)])
    upper = lax.axis_index("zh")
    ring = jnp.where(upper == 0, jnp.concatenate([ring, other], axis=0), jnp.concatenate([other, ring], axis=0))
    chunks = ring.shape[0]
    ring = ring.reshape(chunks, per, fields, cells)
    ring = jnp.concatenate([ring[..., lag:], jnp.roll(ring, -1, axis=0)[..., :lag]], axis=-1)
    me = lax.axis_index("xy")
    per_chunk = cells // BLOCK
    count = chunks * per_chunk
    doubled = jnp.concatenate([ring, ring], axis=0)
    groups = [list(range(per))] if n_half % radii == 0 else [[t] for t in range(per)]
    mine = []
    for group in groups:
        line = doubled[:, group[0] : group[-1] + 1]
        lane = lax.broadcasted_iota(jnp.int32, (n_half,) + line.shape[1:], line.ndim - 1)
        shift = lax.dynamic_index_in_dim(shift_row, first_row + (group[0] * n_half + me) % radii, keepdims=False)
        shift = shift % count
        whole = shift // per_chunk
        part = shift % per_chunk
        base = lax.dynamic_slice_in_dim(line, (chunks - whole + upper * n_half) % chunks, n_half, 0)
        earlier = lax.dynamic_slice_in_dim(line, (chunks - whole - 1 + upper * n_half) % chunks, n_half, 0)
        rolled = base
        for step in range(1, per_chunk):
            mixed = jnp.roll(jnp.where(lane < cells - step * BLOCK, base, earlier), step * BLOCK, axis=-1)
            rolled = jnp.where(part == step, mixed, rolled)
        mine.append(rolled)
    out = jnp.concatenate(mine, axis=1).reshape(n_half, per * fields, cells)
    back = lax.all_to_all(out, "xy", 0, 0, tiled=True).reshape(n_half, per, fields, cells)
    back = jnp.swapaxes(back, 0, 1).reshape(n_lines, fields, cells)
    return jnp.swapaxes(back, 0, 1).reshape(fields, heights, radii, cells)


def body(fields, viscosity, rotation, shift_blocks):
    n_f, heights, radii, cells = fields.shape
    w = HALO
    band = lax.axis_index("rad")
    first_row = band * radii
    total_rows = rotation.shape[0]
    packed = jnp.concatenate([fields.reshape(n_f * heights, radii, cells), viscosity[None]], axis=0)
    tail = jnp.concatenate(
        [fields[..., cells - 2 * w :].reshape(n_f * heights, radii, 2 * w), viscosity[None, :, cells - 2 * w :]], axis=0
    )
    ext = exchange_halo(packed, tail, w)
    u0 = ext[: n_f * heights].reshape(n_f, heights, radii + 2 * w, cells + 2 * w)
    visc = ext[n_f * heights]
    rot = jnp.concatenate([jnp.zeros((w,), rotation.dtype), rotation, jnp.zeros((w,), rotation.dtype)])
    spin = lax.dynamic_slice_in_dim(rot, first_row, radii + 2 * w)[:, None]
    row = first_row - w + lax.iota(jnp.int32, radii + 2 * w)
    inside = ((row >= 0) & (row < total_rows))[:, None]

    def trim(x, k):
        return x[..., k : x.shape[-2] - k, k : x.shape[-1] - k]

    def rates_at(state, k):
        return rates(state, trim(visc, k), spin[k : spin.shape[0] - k])

    def keep(state, k):
        return jnp.where(inside[k : inside.shape[0] - k], state, 0.0)

    state = u0
    first = keep(trim(state, 1) + time_step * rates_at(state, 1), 1)
    second = keep(0.75 * trim(state, 2) + 0.25 * (trim(first, 1) + time_step * rates_at(first, 2)), 2)
    state = trim(state, 3) / 3.0 + 2.0 / 3.0 * (trim(second, 1) + time_step * rates_at(second, 3))
    for t in range(shift_blocks.shape[0]):
        state = advect(state, shift_blocks[t], first_row, w)
    return state


def solution(mesh):
    n_r, n_a = mesh.devices.shape
    halves = Mesh(mesh.devices.reshape(n_r, 2, n_a // 2), ("rad",) + AZI)
    return jax.shard_map(
        body,
        mesh=halves,
        in_specs=(P(None, None, "rad", AZI), P("rad", AZI), P(), P()),
        out_specs=P(None, None, "rad", AZI),
        check_vma=False,
    )
```
